32 devices in a mesh: dp: 8 (over y, x, core), ctx: 4 (over z).
Axes of the slice: x: 2, y: 2, z: 4, core: 2. Of those that a mesh axis runs over, the one named last changes fastest.
Arguments:
- inputs: bfloat16 [16, 1024, 768], P('dp', 'ctx'), may hold values from -6 to 6
- lengths: int32 [16], P('dp'), may hold values from 921 to 1024, as said below
- ln1_gain: bfloat16 [768], P(('dp', 'ctx')), may hold values from 0.5 to 1.5
- ln1_bias: bfloat16 [768], P(('dp', 'ctx')), may hold values from -4 to 4
- query_weight: bfloat16 [768, 768], P(('dp', 'ctx')), may hold values from -0.3125 to 0.3125
- query_bias: bfloat16 [768], P(('dp', 'ctx')), may hold values from -4 to 4
- key_weight: bfloat16 [768, 768], P(('dp', 'ctx')), may hold values from -0.3125 to 0.3125
- value_weight: bfloat16 [768, 768], P(('dp', 'ctx')), may hold values from -0.21875 to 0.21875
- value_bias: bfloat16 [768], P(('dp', 'ctx')), may hold values from -0.75 to 0.75
- out_weight: bfloat16 [768, 768], P(('dp', 'ctx')), may hold values from -1.75 to 1.75
- out_bias: bfloat16 [768], P(('dp', 'ctx')), may hold values from -4 to 4
- ln2_gain: bfloat16 [768], P(('dp', 'ctx')), may hold values from 0.5 to 1.5
- ln2_bias: bfloat16 [768], P(('dp', 'ctx')), may hold values from -4 to 4
- ffn_in_weight: bfloat16 [768, 3072], P(('dp', 'ctx')), may hold values from -0.21875 to 0.21875
- ffn_in_bias: bfloat16 [3072], P(('dp', 'ctx')), may hold values from -4 to 4
- ffn_out_weight: bfloat16 [3072, 768], P(('dp', 'ctx')), may hold values from -0.15625 to 0.15625
- ffn_out_bias: bfloat16 [768], P(('dp', 'ctx')), may hold values from -4 to 4
- out_grad: bfloat16 [16, 1024, 768], P('dp', 'ctx'), may hold values from -6 to 6
Outputs:
- output: bfloat16 [16, 1024, 768], P('dp', 'ctx')
- input_grad: bfloat16 [16, 1024, 768], P('dp', 'ctx')
- grad_ln1_gain: float32 [768], P(('dp', 'ctx'))
- grad_ln1_bias: float32 [768], P(('dp', 'ctx'))
- grad_query: float32 [768, 768], P(('dp', 'ctx'))
- grad_query_bias: float32 [768], P(('dp', 'ctx'))
- grad_key: float32 [768, 768], P(('dp', 'ctx'))
- grad_value: float32 [768, 768], P(('dp', 'ctx'))
- grad_value_bias: float32 [768], P(('dp', 'ctx'))
- grad_out: float32 [768, 768], P(('dp', 'ctx'))
- grad_out_bias: float32 [768], P(('dp', 'ctx'))
- grad_ln2_gain: float32 [768], P(('dp', 'ctx'))
- grad_ln2_bias: float32 [768], P(('dp', 'ctx'))
- grad_ffn_in: float32 [768, 3072], P(('dp', 'ctx'))
- grad_ffn_in_bias: float32 [3072], P(('dp', 'ctx'))
- grad_ffn_out: float32 [3072, 768], P(('dp', 'ctx'))
- grad_ffn_out_bias: float32 [768], P(('dp', 'ctx'))
The draws below stay inside these ranges and needn't reach their ends.
Inputs may be any that keep to these rules, and one draw needn't show every extreme that they name: `lengths`: A sequence's molecules occupy positions 0 to its length - 1; some sequence has exactly 1024, some exactly 921.
All inputs are finite; a program needn't handle non-finite values.
Results may differ from the reference program's by a relative error of at most 0.015.
Values may be sent and summed in bfloat16 or wider, within the bound.
No kernel may reach another device: no remote copies, remote signals or barrier semaphores. Data moves between devices by JAX's collectives and lax.ppermute only.
A program may use at most 192 MiB of HBM per device.

```python
import jax
import jax.numpy as jnp
from jax import lax

D = 768
H = 12
HD = 64
FF = 3072
LEN = 1024
SEQS = 16


def draw_lengths(key, part):
    lowest = 9 * LEN // 10
    first_key, second_key, third_key = jax.random.split(jax.random.fold_in(key, 17), 3)
    drawn = jax.random.randint(first_key, (SEQS,), lowest, LEN + 1)
    longest = jax.random.randint(second_key, (), 0, SEQS)
    shortest = (longest + 1 + jax.random.randint(third_key, (), 0, SEQS - 1)) % SEQS
    drawn = drawn.at[longest].set(LEN).at[shortest].set(lowest)
    return drawn.astype(jnp.int32)


def shard_levels(rng, dims, cuts, low, top_value):
    loudness, own = 1.0, jax.random.fold_in(rng, 6)
    for dim, blocks in cuts:
        heights = jnp.exp(jax.random.uniform(jax.random.fold_in(own, dim), (blocks,), jnp.float32, low / len(cuts), top_value / len(cuts)))
        loudness = loudness * jnp.repeat(heights, dims[dim] // blocks).reshape([-1 if axis == dim else 1 for axis in range(len(dims))])
    return loudness


def normal_values(stream_key, extent, scale, most, cuts=(), held_as=jnp.bfloat16):
    level = shard_levels(stream_key, extent, cuts, -0.22, 0.18) if cuts else 1.0
    values = jax.random.normal(stream_key, extent, jnp.float32) * scale * level
    return jnp.minimum(jnp.maximum(values, -most), most).astype(held_as)


def setup_inputs(seed: int = 0) -> dict:
    splits = jax.random.split(jax.random.key(seed), 19)
    return {
        "inputs": normal_values(splits[0], (SEQS, LEN, D), 1.0, 6.0, ((0, 8), (1, 4))),
        "lengths": draw_lengths(jax.random.fold_in(splits[18], 71), 0),
        "ln1_gain": jnp.clip(1.0 + 0.1 * jax.random.normal(splits[2], (D,), jnp.float32), 0.5, 1.5).astype(jnp.bfloat16),
        "ln1_bias": normal_values(splits[3], (D,), 0.3, 4.0, ((0, 32),)),
        "query_weight": normal_values(splits[4], (D, D), (D // 2) ** -0.5, 0.3125, ((0, 32),)),
        "query_bias": normal_values(splits[5], (D,), 0.3, 4.0, ((0, 32),)),
        "key_weight": normal_values(splits[6], (D, D), (D // 2) ** -0.5, 0.3125, ((0, 32),)),
        "value_weight": normal_values(splits[7], (D, D), D ** -0.5, 0.21875, ((0, 32),)),
        "value_bias": normal_values(splits[8], (D,), 0.05, 0.75, ((0, 32),)),
        "out_weight": normal_values(splits[9], (D, D), (D // 64) ** -0.5, 1.75, ((0, 32),)),
        "out_bias": normal_values(splits[10], (D,), 0.3, 4.0, ((0, 32),)),
        "ln2_gain": jnp.clip(1.0 + 0.1 * jax.random.normal(splits[11], (D,), jnp.float32), 0.5, 1.5).astype(jnp.bfloat16),
        "ln2_bias": normal_values(splits[12], (D,), 0.3, 4.0, ((0, 32),)),
        "ffn_in_weight": normal_values(splits[13], (D, FF), D ** -0.5, 0.21875, ((0, 32),)),
        "ffn_in_bias": normal_values(splits[14], (FF,), 0.3, 4.0, ((0, 32),)),
        "ffn_out_weight": normal_values(splits[15], (FF, D), (FF // 2) ** -0.5, 0.15625, ((0, 32),)),
        "ffn_out_bias": normal_values(splits[16], (D,), 0.3, 4.0, ((0, 32),)),
        "out_grad": normal_values(splits[17], (SEQS, LEN, D), 1.0, 6.0, ((0, 8), (1, 4))),
    }


@jax.custom_vjp
def low(v):
    return lax.optimization_barrier(v.astype(jnp.bfloat16)).astype(jnp.float32)

@jax.custom_vjp
def low_back(v):
    return v

def low_keep(v):
    return (low(v), None)

def low_pass(kept, grad):
    return (grad,)

def back_keep(v):
    return (v, None)

def back_low(kept, grad):
    return (low(grad),)
low.defvjp(low_keep, low_pass)
low_back.defvjp(back_keep, back_low)

def layer_norm(tok_rows, gain, shift):
    center = tok_rows - lax.optimization_barrier(jnp.mean(tok_rows, axis=-1, keepdims=True))
    spread = lax.optimization_barrier(jnp.mean(center * center, axis=-1, keepdims=True))
    return center * lax.rsqrt(spread + 1e-06) * gain + shift

def matmul(left_side, right_side):
    return jnp.dot(left_side, right_side, precision=lax.Precision.HIGHEST, preferred_element_type=jnp.float32)

def seq_layer(tok_rows, length, params):
    ln1_gain, ln1_bias, query_weight, query_bias, key_weight, value_weight, value_bias, out_weight, out_bias, ln2_gain, ln2_bias, ffn_in_weight, ffn_in_bias, ffn_out_weight, ffn_out_bias = params
    seq_len = tok_rows.shape[0]
    normed = low(layer_norm(tok_rows, ln1_gain, ln1_bias))
    queries = low(low_back(matmul(normed, query_weight) + query_bias)).reshape(seq_len, H, HD)
    key_rows = low(low_back(matmul(normed, key_weight))).reshape(seq_len, H, HD)
    value_rows = low(low_back(matmul(normed, value_weight) + value_bias)).reshape(seq_len, H, HD)
    scores = jnp.einsum('qhd,khd->hqk', queries, key_rows, precision=lax.Precision.HIGHEST)
    scores = low_back(scores * HD ** (-0.5))
    valid = jnp.arange(seq_len) < length
    scores = jnp.where(valid[None, None, :], scores, -1e+30)
    attn_probs = low(jax.nn.softmax(scores, axis=-1))
    mixed_rows = jnp.einsum('hqk,khd->qhd', attn_probs, value_rows, precision=lax.Precision.HIGHEST)
    mixed_rows = low(low_back(mixed_rows.reshape(seq_len, H * HD)))
    middle = tok_rows + low_back(matmul(mixed_rows, out_weight) + out_bias)
    normed_two = low(layer_norm(middle, ln2_gain, ln2_bias))
    ffn_pre = low_back(matmul(normed_two, ffn_in_weight) + ffn_in_bias)
    ffn_act = low(jax.nn.gelu(ffn_pre, approximate=False))
    return middle + low_back(matmul(ffn_act, ffn_out_weight) + ffn_out_bias)

def reference(inputs, lengths, ln1_gain, ln1_bias, query_weight, query_bias, key_weight, value_weight, value_bias, out_weight, out_bias, ln2_gain, ln2_bias, ffn_in_weight, ffn_in_bias, ffn_out_weight, ffn_out_bias, out_grad):
    weights_in = (ln1_gain, ln1_bias, query_weight, query_bias, key_weight, value_weight, value_bias, out_weight, out_bias, ln2_gain, ln2_bias, ffn_in_weight, ffn_in_bias, ffn_out_weight, ffn_out_bias)
    params = tuple((weight_item.astype(jnp.float32) for weight_item in weights_in))

    def one_sequence(totals, seq_entry):
        tok_rows, length, cotangent = seq_entry

        def forward(row_values, param_set):
            return seq_layer(row_values, length, param_set)
        result, pullback = jax.vjp(forward, tok_rows.astype(jnp.float32), params)
        d_rows, d_params = pullback(cotangent.astype(jnp.float32))
        totals = jax.tree.map(jnp.add, totals, d_params)
        return (totals, (result.astype(jnp.bfloat16), d_rows.astype(jnp.bfloat16)))
    zero_grads = tuple((jnp.zeros(param_item.shape, jnp.float32) for param_item in params))
    totals, outs_pair = lax.scan(one_sequence, zero_grads, (inputs, lengths, out_grad))
    return (outs_pair[0], outs_pair[1], totals[0], totals[1], totals[2], totals[3], totals[4], totals[5], totals[6], totals[7], totals[8], totals[9], totals[10], totals[11], totals[12], totals[13], totals[14])
```

```python
import math

import jax
import jax.numpy as jnp
from jax import lax
from jax.sharding import PartitionSpec as P

H = 12
HD = 64
EPS = 1e-06
ALL = ("dp", "ctx")


def row_stats(rows):
    mean = jnp.mean(rows, axis=-1, keepdims=True)
    center = rows - mean
    rstd = lax.rsqrt(jnp.mean(center * center, axis=-1, keepdims=True) + EPS)
    return center * rstd, rstd


def norm_back(d_normed, xhat, rstd, gain):
    e = d_normed * gain
    mean_e = jnp.mean(e, axis=-1, keepdims=True)
    mean_ex = jnp.mean(e * xhat, axis=-1, keepdims=True)
    d_rows = (e - mean_e - xhat * mean_ex) * rstd
    return d_rows, jnp.sum(d_normed * xhat, axis=0), jnp.sum(d_normed, axis=0)


def mm(left, right):
    return jnp.dot(left, right, preferred_element_type=jnp.float32)


def outer(left_rows, right_rows):
    return lax.dot_general(
        left_rows, right_rows, (((0,), (0,)), ((), ())), preferred_element_type=jnp.float32
    )


def back(grad_rows, weight):
    return lax.dot_general(
        grad_rows, weight, (((1,), (1,)), ((), ())), preferred_element_type=jnp.float32
    )


def col_sum(rows):
    return jnp.sum(rows.astype(jnp.float32), axis=0)


def pack(pieces, sub):
    flat = jnp.concatenate([p.reshape(-1) for p in pieces])
    size = flat.shape[0]
    padded = -(-size // (sub * 128)) * sub * 128
    flat = jnp.pad(flat, (0, padded - size))
    return flat.reshape(sub, padded // sub)


def gather_all(shards, groups):
    sub = 16
    full = lax.all_gather(pack(shards, sub), ALL, axis=0, tiled=True).reshape(groups, -1)
    out, off = [], 0
    for s in shards:
        size = s.size
        piece = full[:, off:off + size].reshape((groups * s.shape[0],) + s.shape[1:])
        out.append(piece)
        off += size
    return out


def scatter_all(grads, groups):
    sub = 8
    parts = [g.reshape(groups, -1) for g in grads]
    flat = jnp.concatenate(parts, axis=1)
    size = flat.shape[1]
    padded = -(-size // (sub * 128)) * sub * 128
    flat = jnp.pad(flat, ((0, 0), (0, padded - size))).reshape(groups, sub, padded // sub)
    mine = lax.psum_scatter(flat, ALL, scatter_dimension=0, tiled=True).reshape(-1)
    out, off = [], 0
    for g in grads:
        size = g.size // groups
        out.append(mine[off:off + size].reshape((g.shape[0] // groups,) + g.shape[1:]))
        off += size
    return out


def per_device(inputs, lengths, *rest):
    shards = rest[:15]
    out_grad = rest[15]
    groups = lax.axis_size(ALL)
    (ln1_gain, ln1_bias, wq, bq, wk, wv, bv, wo, bo, ln2_gain, ln2_bias, wi, bi, wf, bf) = gather_all(
        shards, groups
    )
    f32 = lambda a: a.astype(jnp.float32)
    seqs, rows, width = inputs.shape
    n = seqs * rows
    x = f32(inputs).reshape(n, width)

    xhat1, rstd1 = row_stats(x)
    normed = (xhat1 * f32(ln1_gain) + f32(ln1_bias)).astype(jnp.bfloat16)
    q = (mm(normed, wq) + f32(bq)).astype(jnp.bfloat16)
    k = mm(normed, wk).astype(jnp.bfloat16)
    v = (mm(normed, wv) + f32(bv)).astype(jnp.bfloat16)
    k_all = lax.all_gather(k.reshape(seqs, rows, width), "ctx", axis=1, tiled=True)
    v_all = lax.all_gather(v.reshape(seqs, rows, width), "ctx", axis=1, tiled=True)
    total = k_all.shape[1]
    qh = q.reshape(seqs, rows, H, HD)
    kh = k_all.reshape(seqs, total, H, HD)
    vh = v_all.reshape(seqs, total, H, HD)
    scale = HD ** (-0.5)
    scores = jnp.einsum("sqhd,skhd->shqk", qh, kh, preferred_element_type=jnp.float32) * scale
    valid = jnp.arange(total)[None, :] < lengths[:, None]
    scores = jnp.where(valid[:, None, None, :], scores, -1e30)
    top = jnp.max(scores, axis=-1, keepdims=True)
    expd = jnp.exp(scores - top)
    probs = expd / jnp.sum(expd, axis=-1, keepdims=True)
    low_probs = probs.astype(jnp.bfloat16)
    mixed = jnp.einsum("shqk,skhd->sqhd", low_probs, vh, preferred_element_type=jnp.float32)
    mixed = mixed.reshape(n, width).astype(jnp.bfloat16)
    middle = x + mm(mixed, wo) + f32(bo)
    xhat2, rstd2 = row_stats(middle)
    normed_two = (xhat2 * f32(ln2_gain) + f32(ln2_bias)).astype(jnp.bfloat16)
    ffn_pre = mm(normed_two, wi) + f32(bi)
    cdf = 0.5 * (1.0 + lax.erf(ffn_pre * (1.0 / math.sqrt(2.0))))
    ffn_act = (ffn_pre * cdf).astype(jnp.bfloat16)
    result = middle + mm(ffn_act, wf) + f32(bf)
    output = result.astype(jnp.bfloat16).reshape(seqs, rows, width)

    g = f32(out_grad).reshape(n, width)
    g_low = g.astype(jnp.bfloat16)
    grad_bf = col_sum(g_low)
    grad_wf = outer(ffn_act, g_low)
    d_act = back(g_low, wf)
    pdf = jnp.exp(-0.5 * ffn_pre * ffn_pre) * (1.0 / math.sqrt(2.0 * math.pi))
    d_pre = (d_act * (cdf + ffn_pre * pdf)).astype(jnp.bfloat16)
    grad_bi = col_sum(d_pre)
    grad_wi = outer(normed_two, d_pre)
    d_normed_two = back(d_pre, wi)
    d_mid, grad_ln2_gain, grad_ln2_bias = norm_back(d_normed_two, xhat2, rstd2, f32(ln2_gain))
    d_middle = g + d_mid
    d_branch = d_middle.astype(jnp.bfloat16)
    grad_bo = col_sum(d_branch)
    grad_wo = outer(mixed, d_branch)
    d_mixed = back(d_branch, wo).astype(jnp.bfloat16).reshape(seqs, rows, H, HD)
    d_probs = jnp.einsum("sqhd,skhd->shqk", d_mixed, vh, preferred_element_type=jnp.float32)
    inner = jnp.sum(probs * d_probs, axis=-1, keepdims=True)
    d_scores = (probs * (d_probs - inner)).astype(jnp.bfloat16)
    d_q = jnp.einsum("shqk,skhd->sqhd", d_scores, kh, preferred_element_type=jnp.float32) * scale
    d_q = d_q.reshape(n, width).astype(jnp.bfloat16)
    k_terms = jnp.einsum("shqk,sqhd->skhd", d_scores, qh, preferred_element_type=jnp.float32) * scale
    v_terms = jnp.einsum("shqk,sqhd->skhd", low_probs, d_mixed, preferred_element_type=jnp.float32)
    d_k = lax.psum_scatter(
        k_terms.reshape(seqs, total, width).astype(jnp.bfloat16), "ctx", scatter_dimension=1, tiled=True
    ).reshape(n, width)
    d_v = lax.psum_scatter(
        v_terms.reshape(seqs, total, width).astype(jnp.bfloat16), "ctx", scatter_dimension=1, tiled=True
    ).reshape(n, width)
    grad_bq = col_sum(d_q)
    grad_bv = col_sum(d_v)
    grad_wq = outer(normed, d_q)
    grad_wk = outer(normed, d_k)
    grad_wv = outer(normed, d_v)
    d_normed = back(d_q, wq) + back(d_k, wk) + back(d_v, wv)
    d_x, grad_ln1_gain, grad_ln1_bias = norm_back(d_normed, xhat1, rstd1, f32(ln1_gain))
    input_grad = (d_middle + d_x).astype(jnp.bfloat16).reshape(seqs, rows, width)

    ffn_part = scatter_all((grad_ln2_gain, grad_ln2_bias, grad_wi, grad_bi), groups)
    ffn_out_part = scatter_all((grad_wf, grad_bf), groups)
    attn_part = scatter_all(
        (grad_ln1_gain, grad_ln1_bias, grad_wq, grad_bq, grad_wk, grad_wv, grad_bv, grad_wo, grad_bo), groups
    )
    return (output, input_grad) + tuple(attn_part) + tuple(ffn_part) + tuple(ffn_out_part)


def solution(mesh):
    row = P(("dp", "ctx"))
    mat = P(("dp", "ctx"), None)
    act = P("dp", "ctx", None)
    weight_specs = (row, row, mat, row, mat, mat, row, mat, row, row, row, mat, row, mat, row)
    return jax.shard_map(
        per_device,
        mesh=mesh,
        in_specs=(act, P("dp")) + weight_specs + (act,),
        out_specs=(act, act) + weight_specs,
        check_vma=False,
    )
```

```python
import math

import jax
import jax.numpy as jnp
from jax import lax
from jax.sharding import PartitionSpec as P

H = 12
HD = 64
EPS = 1e-06
ALL = ("dp", "ctx")


def row_stats(rows):
    mean = jnp.mean(rows, axis=-1, keepdims=True)
    center = rows - mean
    rstd = lax.rsqrt(jnp.mean(center * center, axis=-1, keepdims=True) + EPS)
    return center * rstd, rstd


def norm_back(d_normed, xhat, rstd, gain):
    e = d_normed * gain
    mean_e = jnp.mean(e, axis=-1, keepdims=True)
    mean_ex = jnp.mean(e * xhat, axis=-1, keepdims=True)
    d_rows = (e - mean_e - xhat * mean_ex) * rstd
    return d_rows, jnp.sum(d_normed * xhat, axis=0), jnp.sum(d_normed, axis=0)


def mm(left, right):
    return jnp.dot(left, right, preferred_element_type=jnp.float32)


def outer(left_rows, right_rows):
    return lax.dot_general(
        left_rows, right_rows, (((0,), (0,)), ((), ())), preferred_element_type=jnp.float32
    )


def back(grad_rows, weight):
    return lax.dot_general(
        grad_rows, weight, (((1,), (1,)), ((), ())), preferred_element_type=jnp.float32
    )


def col_sum(rows):
    return jnp.sum(rows.astype(jnp.float32), axis=0)


def pack(pieces, sub):
    flat = jnp.concatenate([p.reshape(-1) for p in pieces])
    size = flat.shape[0]
    padded = -(-size // (sub * 128)) * sub * 128
    flat = jnp.pad(flat, (0, padded - size))
    return flat.reshape(sub, padded // sub)


def gather_all(shards, groups):
    sub = 16
    full = lax.all_gather(pack(shards, sub), ALL, axis=0, tiled=True).reshape(groups, -1)
    out, off = [], 0
    for s in shards:
        size = s.size
        piece = full[:, off:off + size].reshape((groups * s.shape[0],) + s.shape[1:])
        out.append(piece)
        off += size
    return out


def scatter_all(grads, groups):
    sub = 8
    parts = [g.reshape(groups, -1).astype(jnp.bfloat16) for g in grads]
    flat = jnp.concatenate(parts, axis=1)
    size = flat.shape[1]
    padded = -(-size // (sub * 128)) * sub * 128
    flat = jnp.pad(flat, ((0, 0), (0, padded - size))).reshape(groups, sub, padded // sub)
    mine = lax.psum_scatter(flat, ALL, scatter_dimension=0, tiled=True).reshape(-1).astype(jnp.float32)
    out, off = [], 0
    for g in grads:
        size = g.size // groups
        out.append(mine[off:off + size].reshape((g.shape[0] // groups,) + g.shape[1:]))
        off += size
    return out


def per_device(inputs, lengths, *rest):
    shards = rest[:15]
    out_grad = rest[15]
    groups = lax.axis_size(ALL)
    (ln1_gain, ln1_bias, wq, bq, wk, wv, bv, wo, bo, ln2_gain, ln2_bias, wi, bi, wf, bf) = gather_all(
        shards, groups
    )
    f32 = lambda a: a.astype(jnp.float32)
    seqs, rows, width = inputs.shape
    n = seqs * rows
    x = f32(inputs).reshape(n, width)

    xhat1, rstd1 = row_stats(x)
    normed = (xhat1 * f32(ln1_gain) + f32(ln1_bias)).astype(jnp.bfloat16)
    q = (mm(normed, wq) + f32(bq)).astype(jnp.bfloat16)
    k = mm(normed, wk).astype(jnp.bfloat16)
    v = (mm(normed, wv) + f32(bv)).astype(jnp.bfloat16)
    k_all = lax.all_gather(k.reshape(seqs, rows, width), "ctx", axis=1, tiled=True)
    v_all = lax.all_gather(v.reshape(seqs, rows, width), "ctx", axis=1, tiled=True)
    total = k_all.shape[1]
    qh = q.reshape(seqs, rows, H, HD)
    kh = k_all.reshape(seqs, total, H, HD)
    vh = v_all.reshape(seqs, total, H, HD)
    scale = HD ** (-0.5)
    scores = jnp.einsum("sqhd,skhd->shqk", qh, kh, preferred_element_type=jnp.float32) * scale
    valid = jnp.arange(total)[None, :] < lengths[:, None]
    scores = jnp.where(valid[:, None, None, :], scores, -1e30)
    top = jnp.max(scores, axis=-1, keepdims=True)
    expd = jnp.exp(scores - top)
    probs = expd / jnp.sum(expd, axis=-1, keepdims=True)
    low_probs = probs.astype(jnp.bfloat16)
    mixed = jnp.einsum("shqk,skhd->sqhd", low_probs, vh, preferred_element_type=jnp.float32)
    mixed = mixed.reshape(n, width).astype(jnp.bfloat16)
    middle = x + mm(mixed, wo) + f32(bo)
    xhat2, rstd2 = row_stats(middle)
    normed_two = (xhat2 * f32(ln2_gain) + f32(ln2_bias)).astype(jnp.bfloat16)
    ffn_pre = mm(normed_two, wi) + f32(bi)
    cdf = 0.5 * (1.0 + lax.erf(ffn_pre * (1.0 / math.sqrt(2.0))))
    ffn_act = (ffn_pre * cdf).astype(jnp.bfloat16)
    result = middle + mm(ffn_act, wf) + f32(bf)
    output = result.astype(jnp.bfloat16).reshape(seqs, rows, width)

    g = f32(out_grad).reshape(n, width)
    g_low = g.astype(jnp.bfloat16)
    grad_bf = col_sum(g_low)
    grad_wf = outer(ffn_act, g_low)
    d_act = back(g_low, wf)
    pdf = jnp.exp(-0.5 * ffn_pre * ffn_pre) * (1.0 / math.sqrt(2.0 * math.pi))
    d_pre = (d_act * (cdf + ffn_pre * pdf)).astype(jnp.bfloat16)
    grad_bi = col_sum(d_pre)
    grad_wi = outer(normed_two, d_pre)
    d_normed_two = back(d_pre, wi)
    d_mid, grad_ln2_gain, grad_ln2_bias = norm_back(d_normed_two, xhat2, rstd2, f32(ln2_gain))
    d_middle = g + d_mid
    d_branch = d_middle.astype(jnp.bfloat16)
    grad_bo = col_sum(d_branch)
    grad_wo = outer(mixed, d_branch)
    d_mixed = back(d_branch, wo).astype(jnp.bfloat16).reshape(seqs, rows, H, HD)
    d_probs = jnp.einsum("sqhd,skhd->shqk", d_mixed, vh, preferred_element_type=jnp.float32)
    inner = jnp.sum(probs * d_probs, axis=-1, keepdims=True)
    d_scores = (probs * (d_probs - inner)).astype(jnp.bfloat16)
    d_q = jnp.einsum("shqk,skhd->sqhd", d_scores, kh, preferred_element_type=jnp.float32) * scale
    d_q = d_q.reshape(n, width).astype(jnp.bfloat16)
    k_terms = jnp.einsum("shqk,sqhd->skhd", d_scores, qh, preferred_element_type=jnp.float32) * scale
    v_terms = jnp.einsum("shqk,sqhd->skhd", low_probs, d_mixed, preferred_element_type=jnp.float32)
    d_k = lax.psum_scatter(
        k_terms.reshape(seqs, total, width).astype(jnp.bfloat16), "ctx", scatter_dimension=1, tiled=True
    ).reshape(n, width)
    d_v = lax.psum_scatter(
        v_terms.reshape(seqs, total, width).astype(jnp.bfloat16), "ctx", scatter_dimension=1, tiled=True
    ).reshape(n, width)
    grad_bq = col_sum(d_q)
    grad_bv = col_sum(d_v)
    grad_wq = outer(normed, d_q)
    grad_wk = outer(normed, d_k)
    grad_wv = outer(normed, d_v)
    d_normed = back(d_q, wq) + back(d_k, wk) + back(d_v, wv)
    d_x, grad_ln1_gain, grad_ln1_bias = norm_back(d_normed, xhat1, rstd1, f32(ln1_gain))
    input_grad = (d_middle + d_x).astype(jnp.bfloat16).reshape(seqs, rows, width)

    ffn_part = scatter_all((grad_ln2_gain, grad_ln2_bias, grad_wi, grad_bi), groups)
    ffn_out_part = scatter_all((grad_wf, grad_bf), groups)
    attn_part = scatter_all(
        (grad_ln1_gain, grad_ln1_bias, grad_wq, grad_bq, grad_wk, grad_wv, grad_bv, grad_wo, grad_bo), groups
    )
    return (output, input_grad) + tuple(attn_part) + tuple(ffn_part) + tuple(ffn_out_part)


def solution(mesh):
    row = P(("dp", "ctx"))
    mat = P(("dp", "ctx"), None)
    act = P("dp", "ctx", None)
    weight_specs = (row, row, mat, row, mat, mat, row, mat, row, row, row, mat, row, mat, row)
    return jax.shard_map(
        per_device,
        mesh=mesh,
        in_specs=(act, P("dp")) + weight_specs + (act,),
        out_specs=(act, act) + weight_specs,
        check_vma=False,
    )
```

```python
import math

import jax
import jax.numpy as jnp
from jax import lax
from jax.sharding import PartitionSpec as P

H = 12
HD = 64
EPS = 1e-06
ALL = ("dp", "ctx")


def row_stats(rows):
    mean = jnp.mean(rows, axis=-1, keepdims=True)
    center = rows - mean
    rstd = lax.rsqrt(jnp.mean(center * center, axis=-1, keepdims=True) + EPS)
    return center * rstd, rstd


def norm_back(d_normed, xhat, rstd, gain):
    e = d_normed * gain
    mean_e = jnp.mean(e, axis=-1, keepdims=True)
    mean_ex = jnp.mean(e * xhat, axis=-1, keepdims=True)
    d_rows = (e - mean_e - xhat * mean_ex) * rstd
    return d_rows, jnp.sum(d_normed * xhat, axis=0), jnp.sum(d_normed, axis=0)


def mm(left, right):
    return jnp.dot(left, right, preferred_element_type=jnp.float32)


def outer(left_rows, right_rows):
    return lax.dot_general(
        left_rows, right_rows, (((0,), (0,)), ((), ())), preferred_element_type=jnp.float32
    )


def back(grad_rows, weight):
    return lax.dot_general(
        grad_rows, weight, (((1,), (1,)), ((), ())), preferred_element_type=jnp.float32
    )


def col_sum(rows):
    return jnp.sum(rows.astype(jnp.float32), axis=0)


def pack(pieces, sub):
    flat = jnp.concatenate([p.reshape(-1) for p in pieces])
    size = flat.shape[0]
    padded = -(-size // (sub * 128)) * sub * 128
    flat = jnp.pad(flat, (0, padded - size))
    return flat.reshape(sub, padded // sub)


def gather_all(shards, groups):
    sub = 16
    full = lax.all_gather(pack(shards, sub), ALL, axis=0, tiled=True).reshape(groups, -1)
    out, off = [], 0
    for s in shards:
        size = s.size
        piece = full[:, off:off + size].reshape((groups * s.shape[0],) + s.shape[1:])
        out.append(piece)
        off += size
    return out


def scatter_all(grads, mesh_shape):
    groups = mesh_shape[0] * mesh_shape[1]
    sub = 8
    parts = [g.reshape(groups, -1).astype(jnp.bfloat16) for g in grads]
    flat = jnp.concatenate(parts, axis=1)
    size = flat.shape[1]
    padded = -(-size // (sub * 128)) * sub * 128
    flat = jnp.pad(flat, ((0, 0), (0, padded - size)))
    flat = flat.reshape(mesh_shape[0], mesh_shape[1], sub, padded // sub)
    flat = lax.psum_scatter(flat, "dp", scatter_dimension=0, tiled=True)
    mine = lax.psum_scatter(flat, "ctx", scatter_dimension=1, tiled=True).reshape(-1).astype(jnp.float32)
    out, off = [], 0
    for g in grads:
        size = g.size // groups
        out.append(mine[off:off + size].reshape((g.shape[0] // groups,) + g.shape[1:]))
        off += size
    return out


def per_device(inputs, lengths, *rest):
    shards = rest[:15]
    out_grad = rest[15]
    groups = lax.axis_size(ALL)
    (ln1_gain, ln1_bias, wq, bq, wk, wv, bv, wo, bo, ln2_gain, ln2_bias, wi, bi, wf, bf) = gather_all(
        shards, groups
    )
    f32 = lambda a: a.astype(jnp.float32)
    seqs, rows, width = inputs.shape
    n = seqs * rows
    x = f32(inputs).reshape(n, width)

    xhat1, rstd1 = row_stats(x)
    normed = (xhat1 * f32(ln1_gain) + f32(ln1_bias)).astype(jnp.bfloat16)
    q = (mm(normed, wq) + f32(bq)).astype(jnp.bfloat16)
    k = mm(normed, wk).astype(jnp.bfloat16)
    v = (mm(normed, wv) + f32(bv)).astype(jnp.bfloat16)
    k_all = lax.all_gather(k.reshape(seqs, rows, width), "ctx", axis=1, tiled=True)
    v_all = lax.all_gather(v.reshape(seqs, rows, width), "ctx", axis=1, tiled=True)
    total = k_all.shape[1]
    qh = q.reshape(seqs, rows, H, HD)
    kh = k_all.reshape(seqs, total, H, HD)
    vh = v_all.reshape(seqs, total, H, HD)
    scale = HD ** (-0.5)
    scores = jnp.einsum("sqhd,skhd->shqk", qh, kh, preferred_element_type=jnp.float32) * scale
    valid = jnp.arange(total)[None, :] < lengths[:, None]
    scores = jnp.where(valid[:, None, None, :], scores, -1e30)
    top = jnp.max(scores, axis=-1, keepdims=True)
    expd = jnp.exp(scores - top)
    probs = expd / jnp.sum(expd, axis=-1, keepdims=True)
    low_probs = probs.astype(jnp.bfloat16)
    mixed = jnp.einsum("shqk,skhd->sqhd", low_probs, vh, preferred_element_type=jnp.float32)
    mixed = mixed.reshape(n, width).astype(jnp.bfloat16)
    middle = x + mm(mixed, wo) + f32(bo)
    xhat2, rstd2 = row_stats(middle)
    normed_two = (xhat2 * f32(ln2_gain) + f32(ln2_bias)).astype(jnp.bfloat16)
    ffn_pre = mm(normed_two, wi) + f32(bi)
    cdf = 0.5 * (1.0 + lax.erf(ffn_pre * (1.0 / math.sqrt(2.0))))
    ffn_act = (ffn_pre * cdf).astype(jnp.bfloat16)
    result = middle + mm(ffn_act, wf) + f32(bf)
    output = result.astype(jnp.bfloat16).reshape(seqs, rows, width)

    g = f32(out_grad).reshape(n, width)
    g_low = g.astype(jnp.bfloat16)
    grad_bf = col_sum(g_low)
    grad_wf = outer(ffn_act, g_low)
    d_act = back(g_low, wf)
    pdf = jnp.exp(-0.5 * ffn_pre * ffn_pre) * (1.0 / math.sqrt(2.0 * math.pi))
    d_pre = (d_act * (cdf + ffn_pre * pdf)).astype(jnp.bfloat16)
    grad_bi = col_sum(d_pre)
    grad_wi = outer(normed_two, d_pre)
    d_normed_two = back(d_pre, wi)
    d_mid, grad_ln2_gain, grad_ln2_bias = norm_back(d_normed_two, xhat2, rstd2, f32(ln2_gain))
    d_middle = g + d_mid
    d_branch = d_middle.astype(jnp.bfloat16)
    grad_bo = col_sum(d_branch)
    grad_wo = outer(mixed, d_branch)
    d_mixed = back(d_branch, wo).astype(jnp.bfloat16).reshape(seqs, rows, H, HD)
    d_probs = jnp.einsum("sqhd,skhd->shqk", d_mixed, vh, preferred_element_type=jnp.float32)
    inner = jnp.sum(probs * d_probs, axis=-1, keepdims=True)
    d_scores = (probs * (d_probs - inner)).astype(jnp.bfloat16)
    d_q = jnp.einsum("shqk,skhd->sqhd", d_scores, kh, preferred_element_type=jnp.float32) * scale
    d_q = d_q.reshape(n, width).astype(jnp.bfloat16)
    k_terms = jnp.einsum("shqk,sqhd->skhd", d_scores, qh, preferred_element_type=jnp.float32) * scale
    v_terms = jnp.einsum("shqk,sqhd->skhd", low_probs, d_mixed, preferred_element_type=jnp.float32)
    d_k = lax.psum_scatter(
        k_terms.reshape(seqs, total, width).astype(jnp.bfloat16), "ctx", scatter_dimension=1, tiled=True
    ).reshape(n, width)
    d_v = lax.psum_scatter(
        v_terms.reshape(seqs, total, width).astype(jnp.bfloat16), "ctx", scatter_dimension=1, tiled=True
    ).reshape(n, width)
    grad_bq = col_sum(d_q)
    grad_bv = col_sum(d_v)
    grad_wq = outer(normed, d_q)
    grad_wk = outer(normed, d_k)
    grad_wv = outer(normed, d_v)
    d_normed = back(d_q, wq) + back(d_k, wk) + back(d_v, wv)
    d_x, grad_ln1_gain, grad_ln1_bias = norm_back(d_normed, xhat1, rstd1, f32(ln1_gain))
    input_grad = (d_middle + d_x).astype(jnp.bfloat16).reshape(seqs, rows, width)

    grads = (
        grad_ln1_gain,
        grad_ln1_bias,
        grad_wq,
        grad_bq,
        grad_wk,
        grad_wv,
        grad_bv,
        grad_wo,
        grad_bo,
        grad_ln2_gain,
        grad_ln2_bias,
        grad_wi,
        grad_bi,
        grad_wf,
        grad_bf,
    )
    mesh_shape = (lax.axis_size("dp"), lax.axis_size("ctx"))
    return (output, input_grad) + tuple(scatter_all(grads, mesh_shape))


def solution(mesh):
    row = P(("dp", "ctx"))
    mat = P(("dp", "ctx"), None)
    act = P("dp", "ctx", None)
    weight_specs = (row, row, mat, row, mat, mat, row, mat, row, row, row, mat, row, mat, row)
    return jax.shard_map(
        per_device,
        mesh=mesh,
        in_specs=(act, P("dp")) + weight_specs + (act,),
        out_specs=(act, act) + weight_specs,
        check_vma=False,
    )
```

```python
import math

import jax
import jax.numpy as jnp
from jax import lax
from jax.sharding import PartitionSpec as P

H = 12
HD = 64
EPS = 1e-06
ALL = ("dp", "ctx")


def row_stats(rows):
    mean = jnp.mean(rows, axis=-1, keepdims=True)
    center = rows - mean
    rstd = lax.rsqrt(jnp.mean(center * center, axis=-1, keepdims=True) + EPS)
    return center * rstd, rstd


def norm_back_rows(d_normed, xhat, rstd, gain):
    e = d_normed * gain
    mean_e = jnp.mean(e, axis=-1, keepdims=True)
    mean_ex = jnp.mean(e * xhat, axis=-1, keepdims=True)
    return (e - mean_e - xhat * mean_ex) * rstd


def mm(left, right):
    return jnp.dot(left, right, preferred_element_type=jnp.float32)


def outer(left_rows, right_rows):
    return lax.dot_general(
        left_rows, right_rows, (((0,), (0,)), ((), ())), preferred_element_type=jnp.float32
    )


def back(grad_rows, weight):
    return lax.dot_general(
        grad_rows, weight, (((1,), (1,)), ((), ())), preferred_element_type=jnp.float32
    )


def col_sum(rows):
    return jnp.sum(rows.astype(jnp.float32), axis=0)


def round_up(value, step):
    return -(-value // step) * step


MATS = (2, 4, 5, 7, 11, 13)
VECS = (0, 1, 3, 6, 8, 9, 10, 12, 14)


def layout(shards, width, sub):
    rows = [shards[i].size // width for i in MATS]
    vec_len = sum(shards[i].size for i in VECS)
    vec_rows = round_up(vec_len, width) // width
    total = round_up(sum(rows) + vec_rows, sub)
    return rows, vec_len, vec_rows, total


def gather_all(shards, width, groups):
    rows, vec_len, vec_rows, total = layout(shards, width, 16)
    vec = jnp.concatenate([shards[i].reshape(-1) for i in VECS])
    vec = jnp.pad(vec, (0, vec_rows * width - vec_len)).reshape(vec_rows, width)
    blocks = [shards[i].reshape(-1, width) for i in MATS] + [vec]
    packed = jnp.concatenate(blocks, axis=0)
    packed = jnp.pad(packed, ((0, total - packed.shape[0]), (0, 0)))
    full = lax.all_gather(packed[None], ALL, axis=0, tiled=True)
    out = [None] * 15
    off = 0
    for i, r in zip(MATS, rows):
        s = shards[i]
        out[i] = full[:, off:off + r, :].reshape((groups * s.shape[0],) + s.shape[1:])
        off += r
    vecs = full[:, off:off + vec_rows, :].reshape(groups, vec_rows * width)
    voff = 0
    for i in VECS:
        size = shards[i].size
        out[i] = vecs[:, voff:voff + size].reshape(groups * size)
        voff += size
    return out


def scatter_all(grads, width, mesh_shape):
    groups = mesh_shape[0] * mesh_shape[1]
    shard_like = [jnp.zeros((g.shape[0] // groups,) + g.shape[1:], jnp.float32) for g in grads]
    rows, vec_len, vec_rows, total = layout(shard_like, width, 16)
    vec = jnp.concatenate([grads[i].reshape(groups, -1) for i in VECS], axis=1)
    vec = jnp.pad(vec, ((0, 0), (0, vec_rows * width - vec_len))).reshape(groups, vec_rows, width)
    blocks = [grads[i].reshape(groups, -1, width) for i in MATS] + [vec]
    packed = jnp.concatenate([b.astype(jnp.bfloat16) for b in blocks], axis=1)
    packed = jnp.pad(packed, ((0, 0), (0, total - packed.shape[1]), (0, 0)))
    packed = packed.reshape(mesh_shape[0], mesh_shape[1], total, width)
    packed = lax.psum_scatter(packed, "dp", scatter_dimension=0, tiled=True)
    mine = lax.psum_scatter(packed, "ctx", scatter_dimension=1, tiled=True)
    mine = mine.reshape(total, width).astype(jnp.float32)
    out = [None] * 15
    off = 0
    for i, r in zip(MATS, rows):
        out[i] = mine[off:off + r, :].reshape(shard_like[i].shape)
        off += r
    vecs = mine[off:off + vec_rows, :].reshape(-1)
    voff = 0
    for i in VECS:
        size = shard_like[i].size
        out[i] = vecs[voff:voff + size]
        voff += size
    return out


def per_device(inputs, lengths, *rest):
    shards = rest[:15]
    out_grad = rest[15]
    n_ctx = lax.axis_size("ctx")
    mesh_shape = (lax.axis_size("dp"), n_ctx)
    groups = mesh_shape[0] * mesh_shape[1]
    seqs, rows, width = inputs.shape
    f32 = lambda a: a.astype(jnp.float32)

    blocks = [inputs]
    for b in range(1, n_ctx):
        blocks.append(lax.ppermute(inputs, "ctx", [(i, (i + b) % n_ctx) for i in range(n_ctx)]))
    (ln1_gain, ln1_bias, wq, bq, wk, wv, bv, wo, bo, ln2_gain, ln2_bias, wi, bi, wf, bf) = gather_all(
        shards, width, groups
    )
    me = lax.axis_index("ctx")
    total = n_ctx * rows
    source = (me - jnp.arange(n_ctx)) % n_ctx
    positions = (source[:, None] * rows + jnp.arange(rows)[None, :]).reshape(total)
    n = seqs * rows

    x_all = f32(jnp.concatenate(blocks, axis=1)).reshape(seqs * total, width)
    xhat_all, rstd_all = row_stats(x_all)
    normed_all = (xhat_all * f32(ln1_gain) + f32(ln1_bias)).astype(jnp.bfloat16)
    own = lambda a: a.reshape(seqs, total, width)[:, :rows].reshape(n, width)
    normed = own(normed_all)
    xhat1 = own(xhat_all)
    rstd1 = rstd_all.reshape(seqs, total, 1)[:, :rows].reshape(n, 1)
    x = f32(inputs).reshape(n, width)
    q = (mm(normed, wq) + f32(bq)).astype(jnp.bfloat16)
    k = mm(normed_all, wk).astype(jnp.bfloat16)
    v = (mm(normed_all, wv) + f32(bv)).astype(jnp.bfloat16)
    qh = q.reshape(seqs, rows, H, HD)
    kh = k.reshape(seqs, total, H, HD)
    vh = v.reshape(seqs, total, H, HD)
    scale = HD ** (-0.5)
    scores = jnp.einsum("sqhd,skhd->shqk", qh, kh, preferred_element_type=jnp.float32) * scale
    valid = positions[None, :] < lengths[:, None]
    scores = jnp.where(valid[:, None, None, :], scores, -1e30)
    top = jnp.max(scores, axis=-1, keepdims=True)
    expd = jnp.exp(scores - top)
    probs = expd / jnp.sum(expd, axis=-1, keepdims=True)
    low_probs = probs.astype(jnp.bfloat16)
    mixed = jnp.einsum("shqk,skhd->sqhd", low_probs, vh, preferred_element_type=jnp.float32)
    mixed = mixed.reshape(n, width).astype(jnp.bfloat16)
    middle = x + mm(mixed, wo) + f32(bo)
    xhat2, rstd2 = row_stats(middle)
    normed_two = (xhat2 * f32(ln2_gain) + f32(ln2_bias)).astype(jnp.bfloat16)
    ffn_pre = mm(normed_two, wi) + f32(bi)
    cdf = 0.5 * (1.0 + lax.erf(ffn_pre * (1.0 / math.sqrt(2.0))))
    ffn_act = (ffn_pre * cdf).astype(jnp.bfloat16)
    result = middle + mm(ffn_act, wf) + f32(bf)
    output = result.astype(jnp.bfloat16).reshape(seqs, rows, width)

    g = f32(out_grad).reshape(n, width)
    g_low = g.astype(jnp.bfloat16)
    grad_bf = col_sum(g_low)
    grad_wf = outer(ffn_act, g_low)
    d_act = back(g_low, wf)
    pdf = jnp.exp(-0.5 * ffn_pre * ffn_pre) * (1.0 / math.sqrt(2.0 * math.pi))
    d_pre = (d_act * (cdf + ffn_pre * pdf)).astype(jnp.bfloat16)
    grad_bi = col_sum(d_pre)
    grad_wi = outer(normed_two, d_pre)
    d_normed_two = back(d_pre, wi)
    d_mid = norm_back_rows(d_normed_two, xhat2, rstd2, f32(ln2_gain))
    grad_ln2_gain = jnp.sum(d_normed_two * xhat2, axis=0)
    grad_ln2_bias = jnp.sum(d_normed_two, axis=0)
    d_middle = g + d_mid
    d_branch = d_middle.astype(jnp.bfloat16)
    grad_bo = col_sum(d_branch)
    grad_wo = outer(mixed, d_branch)
    d_mixed = back(d_branch, wo).astype(jnp.bfloat16).reshape(seqs, rows, H, HD)
    d_probs = jnp.einsum("sqhd,skhd->shqk", d_mixed, vh, preferred_element_type=jnp.float32)
    inner = jnp.sum(probs * d_probs, axis=-1, keepdims=True)
    d_scores = (probs * (d_probs - inner)).astype(jnp.bfloat16)
    d_q = jnp.einsum("shqk,skhd->sqhd", d_scores, kh, preferred_element_type=jnp.float32) * scale
    d_q = d_q.reshape(n, width).astype(jnp.bfloat16)
    k_part = (
        jnp.einsum("shqk,sqhd->skhd", d_scores, qh, preferred_element_type=jnp.float32) * scale
    ).reshape(seqs * total, width).astype(jnp.bfloat16)
    v_part = jnp.einsum("shqk,sqhd->skhd", low_probs, d_mixed, preferred_element_type=jnp.float32)
    v_part = v_part.reshape(seqs * total, width).astype(jnp.bfloat16)
    grad_bq = col_sum(d_q)
    grad_bv = col_sum(v_part)
    grad_wq = outer(normed, d_q)
    grad_wk = outer(normed_all, k_part)
    grad_wv = outer(normed_all, v_part)
    kv_back = back(k_part, wk) + back(v_part, wv)
    q_back = back(d_q, wq)
    grad_ln1_gain = jnp.sum(kv_back * xhat_all, axis=0) + jnp.sum(q_back * xhat1, axis=0)
    grad_ln1_bias = jnp.sum(kv_back, axis=0) + jnp.sum(q_back, axis=0)

    kv_blocks = kv_back.reshape(seqs, total, width)
    d_normed = kv_blocks[:, :rows] + q_back.reshape(seqs, rows, width)
    for b in range(1, n_ctx):
        sent = kv_blocks[:, b * rows:(b + 1) * rows].astype(jnp.bfloat16)
        got = lax.ppermute(sent, "ctx", [(i, (i - b) % n_ctx) for i in range(n_ctx)])
        d_normed = d_normed + f32(got)
    d_x = norm_back_rows(d_normed.reshape(n, width), xhat1, rstd1, f32(ln1_gain))
    input_grad = (d_middle + d_x).astype(jnp.bfloat16).reshape(seqs, rows, width)

    grads = (
        grad_ln1_gain,
        grad_ln1_bias,
        grad_wq,
        grad_bq,
        grad_wk,
        grad_wv,
        grad_bv,
        grad_wo,
        grad_bo,
        grad_ln2_gain,
        grad_ln2_bias,
        grad_wi,
        grad_bi,
        grad_wf,
        grad_bf,
    )
    return (output, input_grad) + tuple(scatter_all(grads, width, mesh_shape))


def solution(mesh):
    row = P(("dp", "ctx"))
    mat = P(("dp", "ctx"), None)
    act = P("dp", "ctx", None)
    weight_specs = (row, row, mat, row, mat, mat, row, mat, row, row, row, mat, row, mat, row)
    return jax.shard_map(
        per_device,
        mesh=mesh,
        in_specs=(act, P("dp")) + weight_specs + (act,),
        out_specs=(act, act) + weight_specs,
        check_vma=False,
    )
```

```python
import math

import jax
import jax.numpy as jnp
from jax import lax
from jax.sharding import PartitionSpec as P

H = 12
HD = 64
EPS = 1e-06
ALL = ("dp", "ctx")


def row_stats(rows):
    mean = jnp.mean(rows, axis=-1, keepdims=True)
    center = rows - mean
    rstd = lax.rsqrt(jnp.mean(center * center, axis=-1, keepdims=True) + EPS)
    return center * rstd, rstd


def norm_back_rows(d_normed, xhat, rstd, gain):
    e = d_normed * gain
    mean_e = jnp.mean(e, axis=-1, keepdims=True)
    mean_ex = jnp.mean(e * xhat, axis=-1, keepdims=True)
    return (e - mean_e - xhat * mean_ex) * rstd


def mm(left, right):
    return jnp.dot(left, right, preferred_element_type=jnp.float32)


def outer(left_rows, right_rows):
    return lax.dot_general(
        left_rows, right_rows, (((0,), (0,)), ((), ())), preferred_element_type=jnp.float32
    )


def back(grad_rows, weight):
    return lax.dot_general(
        grad_rows, weight, (((1,), (1,)), ((), ())), preferred_element_type=jnp.float32
    )


def col_sum(rows):
    return jnp.sum(rows.astype(jnp.float32), axis=0)


def round_up(value, step):
    return -(-value // step) * step


def layout(shapes, group, width, sub):
    mats = [i for i in group if len(shapes[i]) == 2]
    vecs = [i for i in group if len(shapes[i]) == 1]
    size = lambda i: math.prod(shapes[i])
    rows = [size(i) // width for i in mats]
    vec_len = sum(size(i) for i in vecs)
    vec_rows = round_up(vec_len, width) // width
    total = round_up(sum(rows) + vec_rows, sub)
    return mats, vecs, rows, vec_len, vec_rows, total


def gather_group(shards, group, width, groups):
    shapes = [s.shape for s in shards]
    mats, vecs, rows, vec_len, vec_rows, total = layout(shapes, group, width, 16)
    vec = jnp.concatenate([shards[i].reshape(-1) for i in vecs])
    vec = jnp.pad(vec, (0, vec_rows * width - vec_len)).reshape(vec_rows, width)
    blocks = [shards[i].reshape(-1, width) for i in mats] + [vec]
    spare = total - sum(rows) - vec_rows
    if spare:
        blocks.append(jnp.zeros((spare, width), vec.dtype))
    packed = jnp.concatenate(blocks, axis=0)
    full = lax.all_gather(packed[None], ALL, axis=0, tiled=True)
    out = {}
    off = 0
    for i, r in zip(mats, rows):
        out[i] = full[:, off:off + r, :].reshape((groups * shapes[i][0],) + shapes[i][1:])
        off += r
    flat = full[:, off:off + vec_rows, :].reshape(groups, vec_rows * width)
    voff = 0
    for i in vecs:
        size = shapes[i][0]
        out[i] = flat[:, voff:voff + size].reshape(groups * size)
        voff += size
    return out


def scatter_group(grads, group, width, mesh_shape):
    groups = mesh_shape[0] * mesh_shape[1]
    shapes = {i: (grads[i].shape[0] // groups,) + grads[i].shape[1:] for i in group}
    mats, vecs, rows, vec_len, vec_rows, total = layout(shapes, group, width, 16)
    vec = jnp.concatenate([grads[i].reshape(groups, -1) for i in vecs], axis=1)
    vec = jnp.pad(vec, ((0, 0), (0, vec_rows * width - vec_len))).reshape(groups, vec_rows, width)
    blocks = [grads[i].reshape(groups, -1, width) for i in mats] + [vec]
    spare = total - sum(rows) - vec_rows
    if spare:
        blocks.append(jnp.zeros((groups, spare, width), jnp.float32))
    packed = jnp.concatenate([b.astype(jnp.bfloat16) for b in blocks], axis=1)
    packed = packed.reshape(mesh_shape[0], mesh_shape[1], total, width)
    packed = lax.psum_scatter(packed, "dp", scatter_dimension=0, tiled=True)
    mine = lax.psum_scatter(packed, "ctx", scatter_dimension=1, tiled=True)
    mine = mine.reshape(total, width).astype(jnp.float32)
    out = {}
    off = 0
    for i, r in zip(mats, rows):
        out[i] = mine[off:off + r, :].reshape(shapes[i])
        off += r
    flat = mine[off:off + vec_rows, :].reshape(-1)
    voff = 0
    for i in vecs:
        size = shapes[i][0]
        out[i] = flat[voff:voff + size]
        voff += size
    return out


FIRST = (0, 1, 2, 3, 4, 5, 6)
SECOND = (7, 8, 9, 10, 11, 12, 13, 14)


def per_device(inputs, lengths, *rest):
    shards = rest[:15]
    out_grad = rest[15]
    n_ctx = lax.axis_size("ctx")
    mesh_shape = (lax.axis_size("dp"), n_ctx)
    groups = mesh_shape[0] * mesh_shape[1]
    seqs, rows, width = inputs.shape
    f32 = lambda a: a.astype(jnp.float32)

    blocks = [inputs]
    for b in range(1, n_ctx):
        blocks.append(lax.ppermute(inputs, "ctx", [(i, (i + b) % n_ctx) for i in range(n_ctx)]))
    early = gather_group(shards, FIRST, width, groups)
    late = gather_group(shards, SECOND, width, groups)
    (ln1_gain, ln1_bias, wq, bq, wk, wv, bv) = (early[i] for i in FIRST)
    (wo, bo, ln2_gain, ln2_bias, wi, bi, wf, bf) = (late[i] for i in SECOND)
    me = lax.axis_index("ctx")
    total = n_ctx * rows
    source = (me - jnp.arange(n_ctx)) % n_ctx
    positions = (source[:, None] * rows + jnp.arange(rows)[None, :]).reshape(total)
    n = seqs * rows

    x_all = f32(jnp.concatenate(blocks, axis=1)).reshape(seqs * total, width)
    xhat_all, rstd_all = row_stats(x_all)
    normed_all = (xhat_all * f32(ln1_gain) + f32(ln1_bias)).astype(jnp.bfloat16)
    own = lambda a: a.reshape(seqs, total, width)[:, :rows].reshape(n, width)
    normed = own(normed_all)
    xhat1 = own(xhat_all)
    rstd1 = rstd_all.reshape(seqs, total, 1)[:, :rows].reshape(n, 1)
    x = f32(inputs).reshape(n, width)
    q = (mm(normed, wq) + f32(bq)).astype(jnp.bfloat16)
    k = mm(normed_all, wk).astype(jnp.bfloat16)
    v = (mm(normed_all, wv) + f32(bv)).astype(jnp.bfloat16)
    qh = q.reshape(seqs, rows, H, HD)
    kh = k.reshape(seqs, total, H, HD)
    vh = v.reshape(seqs, total, H, HD)
    scale = HD ** (-0.5)
    scores = jnp.einsum("sqhd,skhd->shqk", qh, kh, preferred_element_type=jnp.float32) * scale
    valid = positions[None, :] < lengths[:, None]
    scores = jnp.where(valid[:, None, None, :], scores, -1e30)
    top = jnp.max(scores, axis=-1, keepdims=True)
    expd = jnp.exp(scores - top)
    probs = expd / jnp.sum(expd, axis=-1, keepdims=True)
    low_probs = probs.astype(jnp.bfloat16)
    mixed = jnp.einsum("shqk,skhd->sqhd", low_probs, vh, preferred_element_type=jnp.float32)
    mixed = mixed.reshape(n, width).astype(jnp.bfloat16)
    middle = x + mm(mixed, wo) + f32(bo)
    xhat2, rstd2 = row_stats(middle)
    normed_two = (xhat2 * f32(ln2_gain) + f32(ln2_bias)).astype(jnp.bfloat16)
    ffn_pre = mm(normed_two, wi) + f32(bi)
    cdf = 0.5 * (1.0 + lax.erf(ffn_pre * (1.0 / math.sqrt(2.0))))
    ffn_act = (ffn_pre * cdf).astype(jnp.bfloat16)
    result = middle + mm(ffn_act, wf) + f32(bf)
    output = result.astype(jnp.bfloat16).reshape(seqs, rows, width)

    g = f32(out_grad).reshape(n, width)
    g_low = g.astype(jnp.bfloat16)
    grad_bf = col_sum(g_low)
    grad_wf = outer(ffn_act, g_low)
    d_act = back(g_low, wf)
    pdf = jnp.exp(-0.5 * ffn_pre * ffn_pre) * (1.0 / math.sqrt(2.0 * math.pi))
    d_pre = (d_act * (cdf + ffn_pre * pdf)).astype(jnp.bfloat16)
    grad_bi = col_sum(d_pre)
    grad_wi = outer(normed_two, d_pre)
    d_normed_two = back(d_pre, wi)
    d_mid = norm_back_rows(d_normed_two, xhat2, rstd2, f32(ln2_gain))
    grad_ln2_gain = jnp.sum(d_normed_two * xhat2, axis=0)
    grad_ln2_bias = jnp.sum(d_normed_two, axis=0)
    d_middle = g + d_mid
    d_branch = d_middle.astype(jnp.bfloat16)
    grad_bo = col_sum(d_branch)
    grad_wo = outer(mixed, d_branch)
    late_grads = dict(
        zip(SECOND, (grad_wo, grad_bo, grad_ln2_gain, grad_ln2_bias, grad_wi, grad_bi, grad_wf, grad_bf))
    )
    late_out = scatter_group(late_grads, SECOND, width, mesh_shape)
    d_mixed = back(d_branch, wo).astype(jnp.bfloat16).reshape(seqs, rows, H, HD)
    d_probs = jnp.einsum("sqhd,skhd->shqk", d_mixed, vh, preferred_element_type=jnp.float32)
    inner = jnp.sum(probs * d_probs, axis=-1, keepdims=True)
    d_scores = (probs * (d_probs - inner)).astype(jnp.bfloat16)
    d_q = jnp.einsum("shqk,skhd->sqhd", d_scores, kh, preferred_element_type=jnp.float32) * scale
    d_q = d_q.reshape(n, width).astype(jnp.bfloat16)
    k_part = (
        jnp.einsum("shqk,sqhd->skhd", d_scores, qh, preferred_element_type=jnp.float32) * scale
    ).reshape(seqs * total, width).astype(jnp.bfloat16)
    v_part = jnp.einsum("shqk,sqhd->skhd", low_probs, d_mixed, preferred_element_type=jnp.float32)
    v_part = v_part.reshape(seqs * total, width).astype(jnp.bfloat16)
    grad_bq = col_sum(d_q)
    grad_bv = col_sum(v_part)
    grad_wq = outer(normed, d_q)
    grad_wk = outer(normed_all, k_part)
    grad_wv = outer(normed_all, v_part)
    kv_back = back(k_part, wk) + back(v_part, wv)
    q_back = back(d_q, wq)
    grad_ln1_gain = jnp.sum(kv_back * xhat_all, axis=0) + jnp.sum(q_back * xhat1, axis=0)
    grad_ln1_bias = jnp.sum(kv_back, axis=0) + jnp.sum(q_back, axis=0)

    kv_blocks = kv_back.reshape(seqs, total, width)
    d_normed = kv_blocks[:, :rows] + q_back.reshape(seqs, rows, width)
    for b in range(1, n_ctx):
        sent = kv_blocks[:, b * rows:(b + 1) * rows].astype(jnp.bfloat16)
        got = lax.ppermute(sent, "ctx", [(i, (i - b) % n_ctx) for i in range(n_ctx)])
        d_normed = d_normed + f32(got)
    d_x = norm_back_rows(d_normed.reshape(n, width), xhat1, rstd1, f32(ln1_gain))
    input_grad = (d_middle + d_x).astype(jnp.bfloat16).reshape(seqs, rows, width)

    early_grads = dict(
        zip(FIRST, (grad_ln1_gain, grad_ln1_bias, grad_wq, grad_bq, grad_wk, grad_wv, grad_bv))
    )
    early_out = scatter_group(early_grads, FIRST, width, mesh_shape)
    return (output, input_grad) + tuple(early_out[i] for i in FIRST) + tuple(late_out[i] for i in SECOND)


def solution(mesh):
    row = P(("dp", "ctx"))
    mat = P(("dp", "ctx"), None)
    act = P("dp", "ctx", None)
    weight_specs = (row, row, mat, row, mat, mat, row, mat, row, row, row, mat, row, mat, row)
    return jax.shard_map(
        per_device,
        mesh=mesh,
        in_specs=(act, P("dp")) + weight_specs + (act,),
        out_specs=(act, act) + weight_specs,
        check_vma=False,
    )
```

```python
import math

import jax
import jax.numpy as jnp
from jax import lax
from jax.sharding import PartitionSpec as P

H = 12
HD = 64
EPS = 1e-06
ALL = ("dp", "ctx")


def row_stats(rows):
    mean = jnp.mean(rows, axis=-1, keepdims=True)
    center = rows - mean
    rstd = lax.rsqrt(jnp.mean(center * center, axis=-1, keepdims=True) + EPS)
    return center * rstd, rstd


def norm_back_rows(d_normed, xhat, rstd, gain):
    e = d_normed * gain
    mean_e = jnp.mean(e, axis=-1, keepdims=True)
    mean_ex = jnp.mean(e * xhat, axis=-1, keepdims=True)
    return (e - mean_e - xhat * mean_ex) * rstd


def mm(left, right):
    return jnp.dot(left, right, preferred_element_type=jnp.float32)


def outer(left_rows, right_rows):
    return lax.dot_general(
        left_rows, right_rows, (((0,), (0,)), ((), ())), preferred_element_type=jnp.float32
    )


def back(grad_rows, weight):
    return lax.dot_general(
        grad_rows, weight, (((1,), (1,)), ((), ())), preferred_element_type=jnp.float32
    )


def col_sum(rows):
    return jnp.sum(rows.astype(jnp.float32), axis=0)


def round_up(value, step):
    return -(-value // step) * step


MATS = (2, 4, 5, 7, 11, 13)
VECS = (0, 1, 3, 6, 8, 9, 10, 12, 14)


def layout(shards, width, sub):
    rows = [shards[i].size // width for i in MATS]
    vec_len = sum(shards[i].size for i in VECS)
    vec_rows = round_up(vec_len, width) // width
    total = round_up(sum(rows) + vec_rows, sub)
    return rows, vec_len, vec_rows, total


def gather_all(shards, width, groups):
    rows, vec_len, vec_rows, total = layout(shards, width, 16)
    vec = jnp.concatenate([shards[i].reshape(-1) for i in VECS])
    vec = jnp.pad(vec, (0, vec_rows * width - vec_len)).reshape(vec_rows, width)
    blocks = [shards[i].reshape(-1, width) for i in MATS] + [vec]
    packed = jnp.concatenate(blocks, axis=0)
    packed = jnp.pad(packed, ((0, total - packed.shape[0]), (0, 0)))
    full = lax.all_gather(packed[None], ALL, axis=0, tiled=True)
    out = [None] * 15
    off = 0
    for i, r in zip(MATS, rows):
        s = shards[i]
        out[i] = full[:, off:off + r, :].reshape((groups * s.shape[0],) + s.shape[1:])
        off += r
    vecs = full[:, off:off + vec_rows, :].reshape(groups, vec_rows * width)
    voff = 0
    for i in VECS:
        size = shards[i].size
        out[i] = vecs[:, voff:voff + size].reshape(groups * size)
        voff += size
    return out


def scatter_all(grads, width, mesh_shape):
    groups = mesh_shape[0] * mesh_shape[1]
    shard_like = [jnp.zeros((g.shape[0] // groups,) + g.shape[1:], jnp.float32) for g in grads]
    rows, vec_len, vec_rows, total = layout(shard_like, width, 16)
    vec = jnp.concatenate([grads[i].reshape(groups, -1) for i in VECS], axis=1)
    spare = total - sum(rows) - vec_rows
    vec = jnp.pad(vec, ((0, 0), (0, (vec_rows + spare) * width - vec_len)))
    vec = vec.reshape(groups, vec_rows + spare, width)
    blocks = [grads[i].reshape(groups, -1, width) for i in MATS] + [vec]
    packed = jnp.concatenate([b.astype(jnp.bfloat16) for b in blocks], axis=1)
    packed = packed.reshape(mesh_shape[0], mesh_shape[1], total, width)
    packed = lax.psum_scatter(packed, "dp", scatter_dimension=0, tiled=True)
    mine = lax.psum_scatter(packed, "ctx", scatter_dimension=1, tiled=True)
    mine = mine.reshape(total, width).astype(jnp.float32)
    out = [None] * 15
    off = 0
    for i, r in zip(MATS, rows):
        out[i] = mine[off:off + r, :].reshape(shard_like[i].shape)
        off += r
    vecs = mine[off:off + vec_rows, :].reshape(-1)
    voff = 0
    for i in VECS:
        size = shard_like[i].size
        out[i] = vecs[voff:voff + size]
        voff += size
    return out


def per_device(inputs, lengths, *rest):
    shards = rest[:15]
    out_grad = rest[15]
    n_ctx = lax.axis_size("ctx")
    mesh_shape = (lax.axis_size("dp"), n_ctx)
    groups = mesh_shape[0] * mesh_shape[1]
    seqs, rows, width = inputs.shape
    f32 = lambda a: a.astype(jnp.float32)

    blocks = [inputs]
    for b in range(1, n_ctx):
        blocks.append(lax.ppermute(inputs, "ctx", [(i, (i + b) % n_ctx) for i in range(n_ctx)]))
    (ln1_gain, ln1_bias, wq, bq, wk, wv, bv, wo, bo, ln2_gain, ln2_bias, wi, bi, wf, bf) = gather_all(
        shards, width, groups
    )
    me = lax.axis_index("ctx")
    total = n_ctx * rows
    source = (me - jnp.arange(n_ctx)) % n_ctx
    positions = (source[:, None] * rows + jnp.arange(rows)[None, :]).reshape(total)
    n = seqs * rows

    x_all = f32(jnp.concatenate(blocks, axis=1)).reshape(seqs * total, width)
    xhat_all, rstd_all = row_stats(x_all)
    normed_all = (xhat_all * f32(ln1_gain) + f32(ln1_bias)).astype(jnp.bfloat16)
    own = lambda a: a.reshape(seqs, total, width)[:, :rows].reshape(n, width)
    normed = own(normed_all)
    xhat1 = own(xhat_all)
    rstd1 = rstd_all.reshape(seqs, total, 1)[:, :rows].reshape(n, 1)
    x = f32(inputs).reshape(n, width)
    q = (mm(normed, wq) + f32(bq)).astype(jnp.bfloat16)
    k = mm(normed_all, wk).astype(jnp.bfloat16)
    v = (mm(normed_all, wv) + f32(bv)).astype(jnp.bfloat16)
    qh = q.reshape(seqs, rows, H, HD)
    kh = k.reshape(seqs, total, H, HD)
    vh = v.reshape(seqs, total, H, HD)
    scale = HD ** (-0.5)
    scores = jnp.einsum("sqhd,skhd->shqk", qh, kh, preferred_element_type=jnp.float32) * scale
    valid = positions[None, :] < lengths[:, None]
    scores = jnp.where(valid[:, None, None, :], scores, -1e30)
    top = jnp.max(scores, axis=-1, keepdims=True)
    expd = jnp.exp(scores - top)
    probs = expd / jnp.sum(expd, axis=-1, keepdims=True)
    low_probs = probs.astype(jnp.bfloat16)
    mixed = jnp.einsum("shqk,skhd->sqhd", low_probs, vh, preferred_element_type=jnp.float32)
    mixed = mixed.reshape(n, width).astype(jnp.bfloat16)
    middle = x + mm(mixed, wo) + f32(bo)
    xhat2, rstd2 = row_stats(middle)
    normed_two = (xhat2 * f32(ln2_gain) + f32(ln2_bias)).astype(jnp.bfloat16)
    ffn_pre = mm(normed_two, wi) + f32(bi)
    cdf = 0.5 * (1.0 + lax.erf(ffn_pre * (1.0 / math.sqrt(2.0))))
    ffn_act = (ffn_pre * cdf).astype(jnp.bfloat16)
    result = middle + mm(ffn_act, wf) + f32(bf)
    output = result.astype(jnp.bfloat16).reshape(seqs, rows, width)

    g = f32(out_grad).reshape(n, width)
    g_low = g.astype(jnp.bfloat16)
    grad_bf = col_sum(g_low)
    grad_wf = outer(ffn_act, g_low)
    d_act = back(g_low, wf)
    pdf = jnp.exp(-0.5 * ffn_pre * ffn_pre) * (1.0 / math.sqrt(2.0 * math.pi))
    d_pre = (d_act * (cdf + ffn_pre * pdf)).astype(jnp.bfloat16)
    grad_bi = col_sum(d_pre)
    grad_wi = outer(normed_two, d_pre)
    d_normed_two = back(d_pre, wi)
    d_mid = norm_back_rows(d_normed_two, xhat2, rstd2, f32(ln2_gain))
    grad_ln2_gain = jnp.sum(d_normed_two * xhat2, axis=0)
    grad_ln2_bias = jnp.sum(d_normed_two, axis=0)
    d_middle = g + d_mid
    d_branch = d_middle.astype(jnp.bfloat16)
    grad_bo = col_sum(d_branch)
    grad_wo = outer(mixed, d_branch)
    d_mixed = back(d_branch, wo).astype(jnp.bfloat16).reshape(seqs, rows, H, HD)
    d_probs = jnp.einsum("sqhd,skhd->shqk", d_mixed, vh, preferred_element_type=jnp.float32)
    inner = jnp.sum(probs * d_probs, axis=-1, keepdims=True)
    d_scores = (probs * (d_probs - inner)).astype(jnp.bfloat16)
    d_q = jnp.einsum("shqk,skhd->sqhd", d_scores, kh, preferred_element_type=jnp.float32) * scale
    d_q = d_q.reshape(n, width).astype(jnp.bfloat16)
    k_part = (
        jnp.einsum("shqk,sqhd->skhd", d_scores, qh, preferred_element_type=jnp.float32) * scale
    ).reshape(seqs * total, width).astype(jnp.bfloat16)
    v_part = jnp.einsum("shqk,sqhd->skhd", low_probs, d_mixed, preferred_element_type=jnp.float32)
    v_part = v_part.reshape(seqs * total, width).astype(jnp.bfloat16)
    grad_bq = col_sum(d_q)
    grad_bv = col_sum(v_part)
    grad_wq = outer(normed, d_q)
    grad_wk = outer(normed_all, k_part)
    grad_wv = outer(normed_all, v_part)
    kv_back = back(k_part, wk) + back(v_part, wv)
    q_back = back(d_q, wq)
    grad_ln1_gain = jnp.sum(kv_back * xhat_all, axis=0) + jnp.sum(q_back * xhat1, axis=0)
    grad_ln1_bias = jnp.sum(kv_back, axis=0) + jnp.sum(q_back, axis=0)

    kv_blocks = kv_back.reshape(seqs, total, width)
    d_normed = kv_blocks[:, :rows] + q_back.reshape(seqs, rows, width)
    for b in range(1, n_ctx):
        sent = kv_blocks[:, b * rows:(b + 1) * rows].astype(jnp.bfloat16)
        got = lax.ppermute(sent, "ctx", [(i, (i - b) % n_ctx) for i in range(n_ctx)])
        d_normed = d_normed + f32(got)
    d_x = norm_back_rows(d_normed.reshape(n, width), xhat1, rstd1, f32(ln1_gain))
    input_grad = (d_middle + d_x).astype(jnp.bfloat16).reshape(seqs, rows, width)

    grads = (
        grad_ln1_gain,
        grad_ln1_bias,
        grad_wq,
        grad_bq,
        grad_wk,
        grad_wv,
        grad_bv,
        grad_wo,
        grad_bo,
        grad_ln2_gain,
        grad_ln2_bias,
        grad_wi,
        grad_bi,
        grad_wf,
        grad_bf,
    )
    return (output, input_grad) + tuple(scatter_all(grads, width, mesh_shape))


def solution(mesh):
    row = P(("dp", "ctx"))
    mat = P(("dp", "ctx"), None)
    act = P("dp", "ctx", None)
    weight_specs = (row, row, mat, row, mat, mat, row, mat, row, row, row, mat, row, mat, row)
    return jax.shard_map(
        per_device,
        mesh=mesh,
        in_specs=(act, P("dp")) + weight_specs + (act,),
        out_specs=(act, act) + weight_specs,
        check_vma=False,
    )
```

```python
import math

import jax
import jax.numpy as jnp
from jax import lax
from jax.sharding import PartitionSpec as P


H = 12
HD = 64
EPS = 1e-06
ALL = ("dp", "ctx")


def row_stats(rows):
    mean = jnp.mean(rows, axis=-1, keepdims=True)
    center = rows - mean
    rstd = lax.rsqrt(jnp.mean(center * center, axis=-1, keepdims=True) + EPS)
    return center * rstd, rstd


def norm_back_rows(d_normed, xhat, rstd, gain):
    e = d_normed * gain
    mean_e = jnp.mean(e, axis=-1, keepdims=True)
    mean_ex = jnp.mean(e * xhat, axis=-1, keepdims=True)
    return (e - mean_e - xhat * mean_ex) * rstd


def mm(left, right):
    return jnp.dot(left, right, preferred_element_type=jnp.float32)


def outer(left_rows, right_rows):
    return lax.dot_general(
        left_rows, right_rows, (((0,), (0,)), ((), ())), preferred_element_type=jnp.float32
    )


def back(grad_rows, weight):
    return lax.dot_general(
        grad_rows, weight, (((1,), (1,)), ((), ())), preferred_element_type=jnp.float32
    )


def col_sum(rows):
    return jnp.sum(rows.astype(jnp.float32), axis=0)


def round_up(value, step):
    return -(-value // step) * step


MATS = (2, 4, 5, 7, 11, 13)
VECS = (0, 1, 3, 6, 8, 9, 10, 12, 14)


def layout(shards, width, sub):
    rows = [shards[i].size // width for i in MATS]
    vec_len = sum(shards[i].size for i in VECS)
    vec_rows = round_up(vec_len, width) // width
    total = round_up(sum(rows) + vec_rows, sub)
    return rows, vec_len, vec_rows, total


def gather_all(shards, width, groups):
    rows, vec_len, vec_rows, total = layout(shards, width, 16)
    vec = jnp.concatenate([shards[i].reshape(-1) for i in VECS])
    vec = jnp.pad(vec, (0, vec_rows * width - vec_len)).reshape(vec_rows, width)
    blocks = [shards[i].reshape(-1, width) for i in MATS] + [vec]
    packed = jnp.concatenate(blocks, axis=0)
    packed = jnp.pad(packed, ((0, total - packed.shape[0]), (0, 0)))
    full = lax.all_gather(packed[None], ALL, axis=0, tiled=True)
    out = [None] * 15
    off = 0
    for i, r in zip(MATS, rows):
        s = shards[i]
        out[i] = full[:, off:off + r, :].reshape((groups * s.shape[0],) + s.shape[1:])
        off += r
    vecs = full[:, off:off + vec_rows, :].reshape(groups, vec_rows * width)
    voff = 0
    for i in VECS:
        size = shards[i].size
        out[i] = vecs[:, voff:voff + size].reshape(groups * size)
        voff += size
    return out


def pack_group(grads, group, width, mesh_shape):
    groups = mesh_shape[0] * mesh_shape[1]
    mats = [i for i in group if grads[i].ndim == 2]
    vecs = [i for i in group if grads[i].ndim == 1]
    rows = [grads[i].size // groups // width for i in mats]
    vec_len = sum(grads[i].size // groups for i in vecs)
    vec_rows = round_up(vec_len, width) // width
    total = round_up(sum(rows) + vec_rows, 16)
    spare = total - sum(rows) - vec_rows
    vec = jnp.concatenate([grads[i].reshape(groups, -1) for i in vecs], axis=1)
    vec = jnp.pad(vec, ((0, 0), (0, (vec_rows + spare) * width - vec_len)))
    vec = vec.reshape(groups, vec_rows + spare, width)
    blocks = [grads[i].reshape(groups, -1, width) for i in mats] + [vec]
    packed = jnp.concatenate([b.astype(jnp.bfloat16) for b in blocks], axis=1)
    return packed.reshape(mesh_shape[0], mesh_shape[1], total, width)


def reduce_group(packed):
    packed = lax.psum_scatter(packed, "dp", scatter_dimension=0, tiled=True)
    mine = lax.psum_scatter(packed, "ctx", scatter_dimension=1, tiled=True)
    return mine.reshape(packed.shape[2], packed.shape[3]).astype(jnp.float32)


def unpack_group(mine, grads, group, width, groups):
    out = {}
    off = 0
    for i in [i for i in group if grads[i].ndim == 2]:
        shape = (grads[i].shape[0] // groups,) + grads[i].shape[1:]
        r = math.prod(shape) // width
        out[i] = mine[off:off + r, :].reshape(shape)
        off += r
    flat = mine[off:, :].reshape(-1)
    voff = 0
    for i in [i for i in group if grads[i].ndim == 1]:
        size = grads[i].shape[0] // groups
        out[i] = flat[voff:voff + size]
        voff += size
    return out


EARLY = (7, 8, 9, 10, 11, 12, 13, 14)
LATE = (0, 1, 2, 3, 4, 5, 6)


def layer(inputs, lengths, *rest):
    shards = rest[:15]
    out_grad = rest[15]
    n_ctx = lax.axis_size("ctx")
    mesh_shape = (lax.axis_size("dp"), n_ctx)
    groups = mesh_shape[0] * mesh_shape[1]
    seqs, rows, width = inputs.shape
    f32 = lambda a: a.astype(jnp.float32)

    blocks = [inputs]
    for b in range(1, n_ctx):
        blocks.append(lax.ppermute(inputs, "ctx", [(i, (i + b) % n_ctx) for i in range(n_ctx)]))
    (ln1_gain, ln1_bias, wq, bq, wk, wv, bv, wo, bo, ln2_gain, ln2_bias, wi, bi, wf, bf) = gather_all(
        shards, width, groups
    )
    me = lax.axis_index("ctx")
    total = n_ctx * rows
    source = (me - jnp.arange(n_ctx)) % n_ctx
    positions = (source[:, None] * rows + jnp.arange(rows)[None, :]).reshape(total)
    n = seqs * rows

    x_all = f32(jnp.concatenate(blocks, axis=1)).reshape(seqs * total, width)
    xhat_all, rstd_all = row_stats(x_all)
    normed_all = (xhat_all * f32(ln1_gain) + f32(ln1_bias)).astype(jnp.bfloat16)
    own = lambda a: a.reshape(seqs, total, width)[:, :rows].reshape(n, width)
    normed = own(normed_all)
    xhat1 = own(xhat_all)
    rstd1 = rstd_all.reshape(seqs, total, 1)[:, :rows].reshape(n, 1)
    x = f32(inputs).reshape(n, width)
    q = (mm(normed, wq) + f32(bq)).astype(jnp.bfloat16)
    k = mm(normed_all, wk).astype(jnp.bfloat16)
    v = (mm(normed_all, wv) + f32(bv)).astype(jnp.bfloat16)
    qh = q.reshape(seqs, rows, H, HD)
    kh = k.reshape(seqs, total, H, HD)
    vh = v.reshape(seqs, total, H, HD)
    scale = HD ** (-0.5)
    scores = jnp.einsum("sqhd,skhd->shqk", qh, kh, preferred_element_type=jnp.float32) * scale
    valid = positions[None, :] < lengths[:, None]
    scores = jnp.where(valid[:, None, None, :], scores, -1e30)
    top = jnp.max(scores, axis=-1, keepdims=True)
    expd = jnp.exp(scores - top)
    probs = expd / jnp.sum(expd, axis=-1, keepdims=True)
    low_probs = probs.astype(jnp.bfloat16)
    mixed = jnp.einsum("shqk,skhd->sqhd", low_probs, vh, preferred_element_type=jnp.float32)
    mixed = mixed.reshape(n, width).astype(jnp.bfloat16)
    middle = x + mm(mixed, wo) + f32(bo)
    xhat2, rstd2 = row_stats(middle)
    normed_two = (xhat2 * f32(ln2_gain) + f32(ln2_bias)).astype(jnp.bfloat16)
    ffn_pre = mm(normed_two, wi) + f32(bi)
    cdf = 0.5 * (1.0 + lax.erf(ffn_pre * (1.0 / math.sqrt(2.0))))
    ffn_act = (ffn_pre * cdf).astype(jnp.bfloat16)
    result = middle + mm(ffn_act, wf) + f32(bf)
    output = result.astype(jnp.bfloat16).reshape(seqs, rows, width)

    g = f32(out_grad).reshape(n, width)
    g_low = g.astype(jnp.bfloat16)
    grad_bf = col_sum(g_low)
    grad_wf = outer(ffn_act, g_low)
    d_act = back(g_low, wf)
    pdf = jnp.exp(-0.5 * ffn_pre * ffn_pre) * (1.0 / math.sqrt(2.0 * math.pi))
    d_pre = (d_act * (cdf + ffn_pre * pdf)).astype(jnp.bfloat16)
    grad_bi = col_sum(d_pre)
    grad_wi = outer(normed_two, d_pre)
    d_normed_two = back(d_pre, wi)
    d_mid = norm_back_rows(d_normed_two, xhat2, rstd2, f32(ln2_gain))
    grad_ln2_gain = jnp.sum(d_normed_two * xhat2, axis=0)
    grad_ln2_bias = jnp.sum(d_normed_two, axis=0)
    d_middle = g + d_mid
    d_branch = d_middle.astype(jnp.bfloat16)
    grad_bo = col_sum(d_branch)
    grad_wo = outer(mixed, d_branch)
    grads = {
        7: grad_wo, 8: grad_bo, 9: grad_ln2_gain, 10: grad_ln2_bias,
        11: grad_wi, 12: grad_bi, 13: grad_wf, 14: grad_bf,
    }
    early_sum = reduce_group(pack_group(grads, EARLY, width, mesh_shape))
    d_mixed = back(d_branch, wo).astype(jnp.bfloat16).reshape(seqs, rows, H, HD)
    d_probs = jnp.einsum("sqhd,skhd->shqk", d_mixed, vh, preferred_element_type=jnp.float32)
    inner = jnp.sum(probs * d_probs, axis=-1, keepdims=True)
    d_scores = (probs * (d_probs - inner)).astype(jnp.bfloat16)
    d_q = jnp.einsum("shqk,skhd->sqhd", d_scores, kh, preferred_element_type=jnp.float32) * scale
    d_q = d_q.reshape(n, width).astype(jnp.bfloat16)
    k_part = (
        jnp.einsum("shqk,sqhd->skhd", d_scores, qh, preferred_element_type=jnp.float32) * scale
    ).reshape(seqs * total, width).astype(jnp.bfloat16)
    v_part = jnp.einsum("shqk,sqhd->skhd", low_probs, d_mixed, preferred_element_type=jnp.float32)
    v_part = v_part.reshape(seqs * total, width).astype(jnp.bfloat16)
    grad_bq = col_sum(d_q)
    grad_bv = col_sum(v_part)
    grad_wq = outer(normed, d_q)
    grad_wk = outer(normed_all, k_part)
    grad_wv = outer(normed_all, v_part)
    kv_back = back(k_part, wk) + back(v_part, wv)
    q_back = back(d_q, wq)
    grad_ln1_gain = jnp.sum(kv_back * xhat_all, axis=0) + jnp.sum(q_back * xhat1, axis=0)
    grad_ln1_bias = jnp.sum(kv_back, axis=0) + jnp.sum(q_back, axis=0)

    kv_blocks = kv_back.reshape(seqs, total, width)
    d_normed = kv_blocks[:, :rows] + q_back.reshape(seqs, rows, width)
    for b in range(1, n_ctx):
        sent = kv_blocks[:, b * rows:(b + 1) * rows].astype(jnp.bfloat16)
        got = lax.ppermute(sent, "ctx", [(i, (i - b) % n_ctx) for i in range(n_ctx)])
        d_normed = d_normed + f32(got)

    grads.update({0: grad_ln1_gain, 1: grad_ln1_bias, 2: grad_wq, 3: grad_bq, 4: grad_wk, 5: grad_wv, 6: grad_bv})
    late_sum = reduce_group(pack_group(grads, LATE, width, mesh_shape))
    xhat1_b, rstd1_b = lax.optimization_barrier((xhat1, rstd1))
    d_x = norm_back_rows(d_normed.reshape(n, width), xhat1_b, rstd1_b, f32(ln1_gain))
    input_grad = (d_middle + d_x).astype(jnp.bfloat16).reshape(seqs, rows, width)
    out = unpack_group(early_sum, grads, EARLY, width, groups)
    out.update(unpack_group(late_sum, grads, LATE, width, groups))
    return (output, input_grad) + tuple(out[i] for i in range(15))


def solution(mesh):
    row = P(("dp", "ctx"))
    mat = P(("dp", "ctx"), None)
    act = P("dp", "ctx", None)
    weight_specs = (row, row, mat, row, mat, mat, row, mat, row, row, row, mat, row, mat, row)
    return jax.shard_map(
        layer,
        mesh=mesh,
        in_specs=(act, P("dp")) + weight_specs + (act,),
        out_specs=(act, act) + weight_specs,
        check_vma=False,
    )
```

```python
import math

import jax
import jax.numpy as jnp
from jax import lax
from jax.sharding import PartitionSpec as P


H = 12
HD = 64
EPS = 1e-06
ALL = ("dp", "ctx")


def row_stats(rows):
    mean = jnp.mean(rows, axis=-1, keepdims=True)
    center = rows - mean
    rstd = lax.rsqrt(jnp.mean(center * center, axis=-1, keepdims=True) + EPS)
    return center * rstd, rstd


def norm_back_rows(d_normed, xhat, rstd, gain):
    e = d_normed * gain
    mean_e = jnp.mean(e, axis=-1, keepdims=True)
    mean_ex = jnp.mean(e * xhat, axis=-1, keepdims=True)
    return (e - mean_e - xhat * mean_ex) * rstd


def mm(left, right):
    return jnp.dot(left, right, preferred_element_type=jnp.float32)


def outer(left_rows, right_rows):
    return lax.dot_general(
        left_rows, right_rows, (((0,), (0,)), ((), ())), preferred_element_type=jnp.float32
    )


def back(grad_rows, weight):
    return lax.dot_general(
        grad_rows, weight, (((1,), (1,)), ((), ())), preferred_element_type=jnp.float32
    )


def col_sum(rows):
    return jnp.sum(rows.astype(jnp.float32), axis=0)


def round_up(value, step):
    return -(-value // step) * step


MATS = (2, 4, 5, 7, 11, 13)
VECS = (0, 1, 3, 6, 8, 9, 10, 12, 14)


def layout(shards, width, sub):
    rows = [shards[i].size // width for i in MATS]
    vec_len = sum(shards[i].size for i in VECS)
    vec_rows = round_up(vec_len, width) // width
    total = round_up(sum(rows) + vec_rows, sub)
    return rows, vec_len, vec_rows, total


def gather_all(shards, width, groups):
    rows, vec_len, vec_rows, total = layout(shards, width, 16)
    vec = jnp.concatenate([shards[i].reshape(-1) for i in VECS])
    vec = jnp.pad(vec, (0, vec_rows * width - vec_len)).reshape(vec_rows, width)
    blocks = [shards[i].reshape(-1, width) for i in MATS] + [vec]
    packed = jnp.concatenate(blocks, axis=0)
    packed = jnp.pad(packed, ((0, total - packed.shape[0]), (0, 0)))
    full = lax.all_gather(packed[None], ALL, axis=0, tiled=True)
    out = [None] * 15
    off = 0
    for i, r in zip(MATS, rows):
        s = shards[i]
        out[i] = full[:, off:off + r, :].reshape((groups * s.shape[0],) + s.shape[1:])
        off += r
    vecs = full[:, off:off + vec_rows, :].reshape(groups, vec_rows * width)
    voff = 0
    for i in VECS:
        size = shards[i].size
        out[i] = vecs[:, voff:voff + size].reshape(groups * size)
        voff += size
    return out


def pack_group(grads, group, width, mesh_shape):
    groups = mesh_shape[0] * mesh_shape[1]
    mats = [i for i in group if grads[i].ndim == 2]
    vecs = [i for i in group if grads[i].ndim == 1]
    rows = [grads[i].size // groups // width for i in mats]
    vec_len = sum(grads[i].size // groups for i in vecs)
    vec_rows = round_up(vec_len, width) // width
    total = round_up(sum(rows) + vec_rows, 16)
    spare = total - sum(rows) - vec_rows
    vec = jnp.concatenate([grads[i].reshape(groups, -1) for i in vecs], axis=1)
    vec = jnp.pad(vec, ((0, 0), (0, (vec_rows + spare) * width - vec_len)))
    vec = vec.reshape(groups, vec_rows + spare, width)
    blocks = [grads[i].reshape(groups, -1, width) for i in mats] + [vec]
    packed = jnp.concatenate([b.astype(jnp.bfloat16) for b in blocks], axis=1)
    return packed.reshape(mesh_shape[0], mesh_shape[1], total, width)


def reduce_group(packed):
    packed = lax.psum_scatter(packed, "dp", scatter_dimension=0, tiled=True)
    mine = lax.psum_scatter(packed, "ctx", scatter_dimension=1, tiled=True)
    return mine.reshape(packed.shape[2], packed.shape[3]).astype(jnp.float32)


def unpack_group(mine, grads, group, width, groups):
    out = {}
    off = 0
    for i in [i for i in group if grads[i].ndim == 2]:
        shape = (grads[i].shape[0] // groups,) + grads[i].shape[1:]
        r = math.prod(shape) // width
        out[i] = mine[off:off + r, :].reshape(shape)
        off += r
    flat = mine[off:, :].reshape(-1)
    voff = 0
    for i in [i for i in group if grads[i].ndim == 1]:
        size = grads[i].shape[0] // groups
        out[i] = flat[voff:voff + size]
        voff += size
    return out


EARLY = (7, 8, 9, 10, 11, 12, 13, 14)
LATE = (0, 1, 2, 3, 4, 5, 6)


def layer(inputs, lengths, *rest):
    shards = rest[:15]
    out_grad = rest[15]
    n_ctx = lax.axis_size("ctx")
    mesh_shape = (lax.axis_size("dp"), n_ctx)
    groups = mesh_shape[0] * mesh_shape[1]
    seqs, rows, width = inputs.shape
    f32 = lambda a: a.astype(jnp.float32)

    blocks = [inputs]
    for b in range(1, n_ctx):
        blocks.append(lax.ppermute(inputs, "ctx", [(i, (i + b) % n_ctx) for i in range(n_ctx)]))
    (ln1_gain, ln1_bias, wq, bq, wk, wv, bv, wo, bo, ln2_gain, ln2_bias, wi, bi, wf, bf) = gather_all(
        shards, width, groups
    )
    me = lax.axis_index("ctx")
    total = n_ctx * rows
    source = (me - jnp.arange(n_ctx)) % n_ctx
    positions = (source[:, None] * rows + jnp.arange(rows)[None, :]).reshape(total)
    n = seqs * rows

    x_all = f32(jnp.concatenate(blocks, axis=1)).reshape(seqs * total, width)
    xhat_all, rstd_all = row_stats(x_all)
    normed_all = (xhat_all * f32(ln1_gain) + f32(ln1_bias)).astype(jnp.bfloat16)
    own = lambda a: a.reshape(seqs, total, width)[:, :rows].reshape(n, width)
    normed = own(normed_all)
    xhat1 = own(xhat_all)
    rstd1 = rstd_all.reshape(seqs, total, 1)[:, :rows].reshape(n, 1)
    x = f32(inputs).reshape(n, width)
    heads = lambda w: w.reshape(width, H, HD)
    project = lambda a, w: jnp.einsum("snd,dhe->shne", a, heads(w), preferred_element_type=jnp.float32)
    own_rows = normed.reshape(seqs, rows, width)
    all_rows = normed_all.reshape(seqs, total, width)
    qh = (project(own_rows, wq) + f32(bq).reshape(H, 1, HD)).astype(jnp.bfloat16)
    kh = project(all_rows, wk).astype(jnp.bfloat16)
    vh = (project(all_rows, wv) + f32(bv).reshape(H, 1, HD)).astype(jnp.bfloat16)
    scale = HD ** (-0.5)
    scores = jnp.einsum("shqd,shkd->shqk", qh, kh, preferred_element_type=jnp.float32) * scale
    valid = positions[None, :] < lengths[:, None]
    scores = jnp.where(valid[:, None, None, :], scores, -1e30)
    top = jnp.max(scores, axis=-1, keepdims=True)
    expd = jnp.exp(scores - top)
    probs = expd / jnp.sum(expd, axis=-1, keepdims=True)
    low_probs = probs.astype(jnp.bfloat16)
    mixed = jnp.einsum("shqk,shkd->sqhd", low_probs, vh, preferred_element_type=jnp.float32)
    mixed = mixed.reshape(n, width).astype(jnp.bfloat16)
    middle = x + mm(mixed, wo) + f32(bo)
    xhat2, rstd2 = row_stats(middle)
    normed_two = (xhat2 * f32(ln2_gain) + f32(ln2_bias)).astype(jnp.bfloat16)
    ffn_pre = mm(normed_two, wi) + f32(bi)
    cdf = 0.5 * (1.0 + lax.erf(ffn_pre * (1.0 / math.sqrt(2.0))))
    ffn_act = (ffn_pre * cdf).astype(jnp.bfloat16)
    result = middle + mm(ffn_act, wf) + f32(bf)
    output = result.astype(jnp.bfloat16).reshape(seqs, rows, width)

    g = f32(out_grad).reshape(n, width)
    g_low = g.astype(jnp.bfloat16)
    grad_bf = col_sum(g_low)
    grad_wf = outer(ffn_act, g_low)
    d_act = back(g_low, wf)
    pdf = jnp.exp(-0.5 * ffn_pre * ffn_pre) * (1.0 / math.sqrt(2.0 * math.pi))
    d_pre = (d_act * (cdf + ffn_pre * pdf)).astype(jnp.bfloat16)
    grad_bi = col_sum(d_pre)
    grad_wi = outer(normed_two, d_pre)
    d_normed_two = back(d_pre, wi)
    d_mid = norm_back_rows(d_normed_two, xhat2, rstd2, f32(ln2_gain))
    grad_ln2_gain = jnp.sum(d_normed_two * xhat2, axis=0)
    grad_ln2_bias = jnp.sum(d_normed_two, axis=0)
    d_middle = g + d_mid
    d_branch = d_middle.astype(jnp.bfloat16)
    grad_bo = col_sum(d_branch)
    grad_wo = outer(mixed, d_branch)
    grads = {
        7: grad_wo, 8: grad_bo, 9: grad_ln2_gain, 10: grad_ln2_bias,
        11: grad_wi, 12: grad_bi, 13: grad_wf, 14: grad_bf,
    }
    early_sum = reduce_group(pack_group(grads, EARLY, width, mesh_shape))
    d_mixed = back(d_branch, wo).astype(jnp.bfloat16).reshape(seqs, rows, H, HD)
    d_probs = jnp.einsum("sqhd,shkd->shqk", d_mixed, vh, preferred_element_type=jnp.float32)
    inner = jnp.sum(probs * d_probs, axis=-1, keepdims=True)
    d_scores = (probs * (d_probs - inner)).astype(jnp.bfloat16)
    d_q = jnp.einsum("shqk,shkd->sqhd", d_scores, kh, preferred_element_type=jnp.float32) * scale
    d_q = d_q.reshape(n, width).astype(jnp.bfloat16)
    k_part = (
        jnp.einsum("shqk,shqd->skhd", d_scores, qh, preferred_element_type=jnp.float32) * scale
    ).reshape(seqs * total, width).astype(jnp.bfloat16)
    v_part = jnp.einsum("shqk,sqhd->skhd", low_probs, d_mixed, preferred_element_type=jnp.float32)
    v_part = v_part.reshape(seqs * total, width).astype(jnp.bfloat16)
    grad_bq = col_sum(d_q)
    grad_bv = col_sum(v_part)
    grad_wq = outer(normed, d_q)
    grad_wk = outer(normed_all, k_part)
    grad_wv = outer(normed_all, v_part)
    kv_back = back(k_part, wk) + back(v_part, wv)
    q_back = back(d_q, wq)
    grad_ln1_gain = jnp.sum(kv_back * xhat_all, axis=0) + jnp.sum(q_back * xhat1, axis=0)
    grad_ln1_bias = jnp.sum(kv_back, axis=0) + jnp.sum(q_back, axis=0)

    kv_blocks = kv_back.reshape(seqs, total, width)
    d_normed = kv_blocks[:, :rows] + q_back.reshape(seqs, rows, width)
    for b in range(1, n_ctx):
        sent = kv_blocks[:, b * rows:(b + 1) * rows].astype(jnp.bfloat16)
        got = lax.ppermute(sent, "ctx", [(i, (i - b) % n_ctx) for i in range(n_ctx)])
        d_normed = d_normed + f32(got)

    grads.update({0: grad_ln1_gain, 1: grad_ln1_bias, 2: grad_wq, 3: grad_bq, 4: grad_wk, 5: grad_wv, 6: grad_bv})
    late_sum = reduce_group(pack_group(grads, LATE, width, mesh_shape))
    xhat1_b, rstd1_b = lax.optimization_barrier((xhat1, rstd1))
    d_x = norm_back_rows(d_normed.reshape(n, width), xhat1_b, rstd1_b, f32(ln1_gain))
    input_grad = (d_middle + d_x).astype(jnp.bfloat16).reshape(seqs, rows, width)
    out = unpack_group(early_sum, grads, EARLY, width, groups)
    out.update(unpack_group(late_sum, grads, LATE, width, groups))
    return (output, input_grad) + tuple(out[i] for i in range(15))


def solution(mesh):
    row = P(("dp", "ctx"))
    mat = P(("dp", "ctx"), None)
    act = P("dp", "ctx", None)
    weight_specs = (row, row, mat, row, mat, mat, row, mat, row, row, row, mat, row, mat, row)
    return jax.shard_map(
        layer,
        mesh=mesh,
        in_specs=(act, P("dp")) + weight_specs + (act,),
        out_specs=(act, act) + weight_specs,
        check_vma=False,
    )
```

```python
import math

import jax
import jax.numpy as jnp
from jax import lax
from jax.sharding import PartitionSpec as P


H = 12
HD = 64
EPS = 1e-06
ALL = ("dp", "ctx")


def row_stats(rows):
    mean = jnp.mean(rows, axis=-1, keepdims=True)
    center = rows - mean
    rstd = lax.rsqrt(jnp.mean(center * center, axis=-1, keepdims=True) + EPS)
    return center * rstd, rstd


def norm_back_rows(d_normed, xhat, rstd, gain):
    e = d_normed * gain
    mean_e = jnp.mean(e, axis=-1, keepdims=True)
    mean_ex = jnp.mean(e * xhat, axis=-1, keepdims=True)
    return (e - mean_e - xhat * mean_ex) * rstd


def mm(left, right):
    return jnp.dot(left, right, preferred_element_type=jnp.float32)


def outer(left_rows, right_rows):
    return lax.dot_general(
        left_rows, right_rows, (((0,), (0,)), ((), ())), preferred_element_type=jnp.float32
    )


def back(grad_rows, weight):
    return lax.dot_general(
        grad_rows, weight, (((1,), (1,)), ((), ())), preferred_element_type=jnp.float32
    )


def col_sum(rows):
    return jnp.sum(rows.astype(jnp.float32), axis=0)


def round_up(value, step):
    return -(-value // step) * step


MATS = (2, 4, 5, 7, 11, 13)
VECS = (0, 1, 3, 6, 8, 9, 10, 12, 14)


def layout(shards, width, sub):
    rows = [shards[i].size // width for i in MATS]
    vec_len = sum(shards[i].size for i in VECS)
    vec_rows = round_up(vec_len, width) // width
    total = round_up(sum(rows) + vec_rows, sub)
    return rows, vec_len, vec_rows, total


def gather_all(shards, width, groups):
    rows, vec_len, vec_rows, total = layout(shards, width, 16)
    vec = jnp.concatenate([shards[i].reshape(-1) for i in VECS])
    vec = jnp.pad(vec, (0, vec_rows * width - vec_len)).reshape(vec_rows, width)
    blocks = [shards[i].reshape(-1, width) for i in MATS] + [vec]
    packed = jnp.concatenate(blocks, axis=0)
    packed = jnp.pad(packed, ((0, total - packed.shape[0]), (0, 0)))
    full = lax.all_gather(packed[None], ALL, axis=0, tiled=True)
    out = [None] * 15
    off = 0
    for i, r in zip(MATS, rows):
        s = shards[i]
        out[i] = full[:, off:off + r, :].reshape((groups * s.shape[0],) + s.shape[1:])
        off += r
    vecs = full[:, off:off + vec_rows, :].reshape(groups, vec_rows * width)
    voff = 0
    for i in VECS:
        size = shards[i].size
        out[i] = vecs[:, voff:voff + size].reshape(groups * size)
        voff += size
    return out


def pack_group(grads, group, width, mesh_shape):
    groups = mesh_shape[0] * mesh_shape[1]
    mats = [i for i in group if grads[i].ndim == 2]
    vecs = [i for i in group if grads[i].ndim == 1]
    rows = [grads[i].size // groups // width for i in mats]
    vec_len = sum(grads[i].size // groups for i in vecs)
    vec_rows = round_up(vec_len, width) // width
    total = round_up(sum(rows) + vec_rows, 16)
    spare = total - sum(rows) - vec_rows
    vec = jnp.concatenate([grads[i].reshape(groups, -1) for i in vecs], axis=1)
    vec = jnp.pad(vec, ((0, 0), (0, (vec_rows + spare) * width - vec_len)))
    vec = vec.reshape(groups, vec_rows + spare, width)
    blocks = [grads[i].reshape(groups, -1, width) for i in mats] + [vec]
    packed = jnp.concatenate([b.astype(jnp.bfloat16) for b in blocks], axis=1)
    return packed.reshape(mesh_shape[0], mesh_shape[1], total, width)


def dp_stage(packed):
    return lax.psum_scatter(packed, "dp", scatter_dimension=0, tiled=True)


def ctx_stage(parts):
    joined = jnp.concatenate(parts, axis=2)
    mine = lax.psum_scatter(joined, "ctx", scatter_dimension=1, tiled=True)
    mine = mine.reshape(joined.shape[2], joined.shape[3]).astype(jnp.float32)
    out, off = [], 0
    for p in parts:
        out.append(mine[off:off + p.shape[2]])
        off += p.shape[2]
    return out


def unpack_group(mine, grads, group, width, groups):
    out = {}
    off = 0
    for i in [i for i in group if grads[i].ndim == 2]:
        shape = (grads[i].shape[0] // groups,) + grads[i].shape[1:]
        r = math.prod(shape) // width
        out[i] = mine[off:off + r, :].reshape(shape)
        off += r
    flat = mine[off:, :].reshape(-1)
    voff = 0
    for i in [i for i in group if grads[i].ndim == 1]:
        size = grads[i].shape[0] // groups
        out[i] = flat[voff:voff + size]
        voff += size
    return out


EARLY = (7, 8, 9, 10, 11, 12, 13, 14)
LATE = (0, 1, 2, 3, 4, 5, 6)


def layer(inputs, lengths, *rest):
    shards = rest[:15]
    out_grad = rest[15]
    n_ctx = lax.axis_size("ctx")
    mesh_shape = (lax.axis_size("dp"), n_ctx)
    groups = mesh_shape[0] * mesh_shape[1]
    seqs, rows, width = inputs.shape
    f32 = lambda a: a.astype(jnp.float32)

    blocks = [inputs]
    for b in range(1, n_ctx):
        blocks.append(lax.ppermute(inputs, "ctx", [(i, (i + b) % n_ctx) for i in range(n_ctx)]))
    (ln1_gain, ln1_bias, wq, bq, wk, wv, bv, wo, bo, ln2_gain, ln2_bias, wi, bi, wf, bf) = gather_all(
        shards, width, groups
    )
    me = lax.axis_index("ctx")
    total = n_ctx * rows
    source = (me - jnp.arange(n_ctx)) % n_ctx
    positions = (source[:, None] * rows + jnp.arange(rows)[None, :]).reshape(total)
    n = seqs * rows

    x_all = f32(jnp.concatenate(blocks, axis=1)).reshape(seqs * total, width)
    xhat_all, rstd_all = row_stats(x_all)
    normed_all = (xhat_all * f32(ln1_gain) + f32(ln1_bias)).astype(jnp.bfloat16)
    own = lambda a: a.reshape(seqs, total, width)[:, :rows].reshape(n, width)
    normed = own(normed_all)
    xhat1 = own(xhat_all)
    rstd1 = rstd_all.reshape(seqs, total, 1)[:, :rows].reshape(n, 1)
    x = f32(inputs).reshape(n, width)
    heads = lambda w: w.reshape(width, H, HD)
    project = lambda a, w: jnp.einsum("snd,dhe->shne", a, heads(w), preferred_element_type=jnp.float32)
    own_rows = normed.reshape(seqs, rows, width)
    all_rows = normed_all.reshape(seqs, total, width)
    qh = (project(own_rows, wq) + f32(bq).reshape(H, 1, HD)).astype(jnp.bfloat16)
    kh = project(all_rows, wk).astype(jnp.bfloat16)
    vh = (project(all_rows, wv) + f32(bv).reshape(H, 1, HD)).astype(jnp.bfloat16)
    scale = HD ** (-0.5)
    scores = jnp.einsum("shqd,shkd->shqk", qh, kh, preferred_element_type=jnp.float32) * scale
    valid = positions[None, :] < lengths[:, None]
    scores = jnp.where(valid[:, None, None, :], scores, -1e30)
    top = jnp.max(scores, axis=-1, keepdims=True)
    expd = jnp.exp(scores - top)
    probs = expd / jnp.sum(expd, axis=-1, keepdims=True)
    low_probs = probs.astype(jnp.bfloat16)
    mixed = jnp.einsum("shqk,shkd->sqhd", low_probs, vh, preferred_element_type=jnp.float32)
    mixed = mixed.reshape(n, width).astype(jnp.bfloat16)
    middle = x + mm(mixed, wo) + f32(bo)
    xhat2, rstd2 = row_stats(middle)
    normed_two = (xhat2 * f32(ln2_gain) + f32(ln2_bias)).astype(jnp.bfloat16)
    ffn_pre = mm(normed_two, wi) + f32(bi)
    cdf = 0.5 * (1.0 + lax.erf(ffn_pre * (1.0 / math.sqrt(2.0))))
    ffn_act = (ffn_pre * cdf).astype(jnp.bfloat16)
    result = middle + mm(ffn_act, wf) + f32(bf)
    output = result.astype(jnp.bfloat16).reshape(seqs, rows, width)

    g = f32(out_grad).reshape(n, width)
    g_low = g.astype(jnp.bfloat16)
    grad_bf = col_sum(g_low)
    grad_wf = outer(ffn_act, g_low)
    d_act = back(g_low, wf)
    pdf = jnp.exp(-0.5 * ffn_pre * ffn_pre) * (1.0 / math.sqrt(2.0 * math.pi))
    d_pre = (d_act * (cdf + ffn_pre * pdf)).astype(jnp.bfloat16)
    grad_bi = col_sum(d_pre)
    grad_wi = outer(normed_two, d_pre)
    d_normed_two = back(d_pre, wi)
    d_mid = norm_back_rows(d_normed_two, xhat2, rstd2, f32(ln2_gain))
    grad_ln2_gain = jnp.sum(d_normed_two * xhat2, axis=0)
    grad_ln2_bias = jnp.sum(d_normed_two, axis=0)
    d_middle = g + d_mid
    d_branch = d_middle.astype(jnp.bfloat16)
    grad_bo = col_sum(d_branch)
    grad_wo = outer(mixed, d_branch)
    grads = {
        7: grad_wo, 8: grad_bo, 9: grad_ln2_gain, 10: grad_ln2_bias,
        11: grad_wi, 12: grad_bi, 13: grad_wf, 14: grad_bf,
    }
    early_part = dp_stage(pack_group(grads, EARLY, width, mesh_shape))
    d_mixed = back(d_branch, wo).astype(jnp.bfloat16).reshape(seqs, rows, H, HD)
    d_probs = jnp.einsum("sqhd,shkd->shqk", d_mixed, vh, preferred_element_type=jnp.float32)
    inner = jnp.sum(probs * d_probs, axis=-1, keepdims=True)
    d_scores = (probs * (d_probs - inner)).astype(jnp.bfloat16)
    d_q = jnp.einsum("shqk,shkd->sqhd", d_scores, kh, preferred_element_type=jnp.float32) * scale
    d_q = d_q.reshape(n, width).astype(jnp.bfloat16)
    k_part = (
        jnp.einsum("shqk,shqd->skhd", d_scores, qh, preferred_element_type=jnp.float32) * scale
    ).reshape(seqs * total, width).astype(jnp.bfloat16)
    v_part = jnp.einsum("shqk,sqhd->skhd", low_probs, d_mixed, preferred_element_type=jnp.float32)
    v_part = v_part.reshape(seqs * total, width).astype(jnp.bfloat16)
    grad_bq = col_sum(d_q)
    grad_bv = col_sum(v_part)
    grad_wq = outer(normed, d_q)
    grad_wk = outer(normed_all, k_part)
    grad_wv = outer(normed_all, v_part)
    kv_back = back(k_part, wk) + back(v_part, wv)
    q_back = back(d_q, wq)
    grad_ln1_gain = jnp.sum(kv_back * xhat_all, axis=0) + jnp.sum(q_back * xhat1, axis=0)
    grad_ln1_bias = jnp.sum(kv_back, axis=0) + jnp.sum(q_back, axis=0)

    kv_blocks = kv_back.reshape(seqs, total, width)
    d_normed = kv_blocks[:, :rows] + q_back.reshape(seqs, rows, width)
    for b in range(1, n_ctx):
        sent = kv_blocks[:, b * rows:(b + 1) * rows].astype(jnp.bfloat16)
        got = lax.ppermute(sent, "ctx", [(i, (i - b) % n_ctx) for i in range(n_ctx)])
        d_normed = d_normed + f32(got)

    grads.update({0: grad_ln1_gain, 1: grad_ln1_bias, 2: grad_wq, 3: grad_bq, 4: grad_wk, 5: grad_wv, 6: grad_bv})
    late_part = dp_stage(pack_group(grads, LATE, width, mesh_shape))
    xhat1_b, rstd1_b = lax.optimization_barrier((xhat1, rstd1))
    d_x = norm_back_rows(d_normed.reshape(n, width), xhat1_b, rstd1_b, f32(ln1_gain))
    input_grad = (d_middle + d_x).astype(jnp.bfloat16).reshape(seqs, rows, width)
    early_sum, late_sum = ctx_stage([early_part, late_part])
    out = unpack_group(early_sum, grads, EARLY, width, groups)
    out.update(unpack_group(late_sum, grads, LATE, width, groups))
    return (output, input_grad) + tuple(out[i] for i in range(15))


def solution(mesh):
    row = P(("dp", "ctx"))
    mat = P(("dp", "ctx"), None)
    act = P("dp", "ctx", None)
    weight_specs = (row, row, mat, row, mat, mat, row, mat, row, row, row, mat, row, mat, row)
    return jax.shard_map(
        layer,
        mesh=mesh,
        in_specs=(act, P("dp")) + weight_specs + (act,),
        out_specs=(act, act) + weight_specs,
        check_vma=False,
    )
```

```python
import math

import jax
import jax.numpy as jnp
from jax import lax
from jax.sharding import PartitionSpec as P


H = 12
HD = 64
EPS = 1e-06
ALL = ("dp", "ctx")


def row_stats(rows):
    mean = jnp.mean(rows, axis=-1, keepdims=True)
    center = rows - mean
    rstd = lax.rsqrt(jnp.mean(center * center, axis=-1, keepdims=True) + EPS)
    return center * rstd, rstd


def norm_back_rows(d_normed, xhat, rstd, gain):
    e = d_normed * gain
    mean_e = jnp.mean(e, axis=-1, keepdims=True)
    mean_ex = jnp.mean(e * xhat, axis=-1, keepdims=True)
    return (e - mean_e - xhat * mean_ex) * rstd


def mm(left, right):
    return jnp.dot(left, right, preferred_element_type=jnp.float32)


def outer(left_rows, right_rows):
    return lax.dot_general(
        left_rows, right_rows, (((0,), (0,)), ((), ())), preferred_element_type=jnp.float32
    )


def back(grad_rows, weight):
    return lax.dot_general(
        grad_rows, weight, (((1,), (1,)), ((), ())), preferred_element_type=jnp.float32
    )


def col_sum(rows):
    return jnp.sum(rows.astype(jnp.float32), axis=0)


def round_up(value, step):
    return -(-value // step) * step


def layout(shards, group, width, sub):
    mats = [i for i in group if shards[i].ndim == 2]
    vecs = [i for i in group if shards[i].ndim == 1]
    rows = [shards[i].size // width for i in mats]
    vec_len = sum(shards[i].size for i in vecs)
    vec_rows = round_up(vec_len, width) // width
    total = round_up(sum(rows) + vec_rows, sub)
    return mats, vecs, rows, vec_len, vec_rows, total


def gather_all(shards, group, width, groups):
    mats, vecs, rows, vec_len, vec_rows, total = layout(shards, group, width, 16)
    spare = total - sum(rows) - vec_rows
    vec = jnp.concatenate([shards[i].reshape(-1) for i in vecs])
    vec = jnp.pad(vec, (0, (vec_rows + spare) * width - vec_len)).reshape(vec_rows + spare, width)
    blocks = [shards[i].reshape(-1, width) for i in mats] + [vec]
    packed = jnp.concatenate(blocks, axis=0)
    full = lax.all_gather(packed[None], ALL, axis=0, tiled=True)
    out = {}
    off = 0
    for i, r in zip(mats, rows):
        s = shards[i]
        out[i] = full[:, off:off + r, :].reshape((groups * s.shape[0],) + s.shape[1:])
        off += r
    flat = full[:, off:off + vec_rows, :].reshape(groups, vec_rows * width)
    voff = 0
    for i in vecs:
        size = shards[i].size
        out[i] = flat[:, voff:voff + size].reshape(groups * size)
        voff += size
    return [out[i] for i in group]


LATE_W = (11, 12, 13, 14)


def pack_group(grads, group, width, mesh_shape):
    groups = mesh_shape[0] * mesh_shape[1]
    mats = [i for i in group if grads[i].ndim == 2]
    vecs = [i for i in group if grads[i].ndim == 1]
    rows = [grads[i].size // groups // width for i in mats]
    vec_len = sum(grads[i].size // groups for i in vecs)
    vec_rows = round_up(vec_len, width) // width
    total = round_up(sum(rows) + vec_rows, 16)
    spare = total - sum(rows) - vec_rows
    vec = jnp.concatenate([grads[i].reshape(groups, -1) for i in vecs], axis=1)
    vec = jnp.pad(vec, ((0, 0), (0, (vec_rows + spare) * width - vec_len)))
    vec = vec.reshape(groups, vec_rows + spare, width)
    blocks = [grads[i].reshape(groups, -1, width) for i in mats] + [vec]
    packed = jnp.concatenate([b.astype(jnp.bfloat16) for b in blocks], axis=1)
    return packed.reshape(mesh_shape[0], mesh_shape[1], total, width)


def dp_stage(packed):
    return lax.psum_scatter(packed, "dp", scatter_dimension=0, tiled=True)


def ctx_stage(parts):
    joined = jnp.concatenate(parts, axis=2)
    mine = lax.psum_scatter(joined, "ctx", scatter_dimension=1, tiled=True)
    mine = mine.reshape(joined.shape[2], joined.shape[3]).astype(jnp.float32)
    out, off = [], 0
    for p in parts:
        out.append(mine[off:off + p.shape[2]])
        off += p.shape[2]
    return out


def unpack_group(mine, grads, group, width, groups):
    out = {}
    off = 0
    for i in [i for i in group if grads[i].ndim == 2]:
        shape = (grads[i].shape[0] // groups,) + grads[i].shape[1:]
        r = math.prod(shape) // width
        out[i] = mine[off:off + r, :].reshape(shape)
        off += r
    flat = mine[off:, :].reshape(-1)
    voff = 0
    for i in [i for i in group if grads[i].ndim == 1]:
        size = grads[i].shape[0] // groups
        out[i] = flat[voff:voff + size]
        voff += size
    return out


EARLY = (7, 8, 9, 10, 11, 12, 13, 14)
LATE = (0, 1, 2, 3, 4, 5, 6)


def layer(inputs, lengths, *rest):
    shards = rest[:15]
    out_grad = rest[15]
    n_ctx = lax.axis_size("ctx")
    mesh_shape = (lax.axis_size("dp"), n_ctx)
    groups = mesh_shape[0] * mesh_shape[1]
    seqs, rows, width = inputs.shape
    f32 = lambda a: a.astype(jnp.float32)

    blocks = [inputs]
    for b in range(1, n_ctx):
        blocks.append(lax.ppermute(inputs, "ctx", [(i, (i + b) % n_ctx) for i in range(n_ctx)]))
    first = (0, 1, 2, 3, 4, 5, 6, 7, 8, 9, 10)
    ln1_gain, ln1_bias, wq, bq, wk, wv, bv, wo, bo, ln2_gain, ln2_bias = gather_all(
        shards, first, width, groups
    )
    wi, bi, wf, bf = gather_all(shards, LATE_W, width, groups)
    me = lax.axis_index("ctx")
    total = n_ctx * rows
    source = (me - jnp.arange(n_ctx)) % n_ctx
    positions = (source[:, None] * rows + jnp.arange(rows)[None, :]).reshape(total)
    n = seqs * rows

    x_all = f32(jnp.concatenate(blocks, axis=1)).reshape(seqs * total, width)
    xhat_all, rstd_all = row_stats(x_all)
    normed_all = (xhat_all * f32(ln1_gain) + f32(ln1_bias)).astype(jnp.bfloat16)
    own = lambda a: a.reshape(seqs, total, width)[:, :rows].reshape(n, width)
    normed = own(normed_all)
    xhat1 = own(xhat_all)
    rstd1 = rstd_all.reshape(seqs, total, 1)[:, :rows].reshape(n, 1)
    x = f32(inputs).reshape(n, width)
    heads = lambda w: w.reshape(width, H, HD)
    project = lambda a, w: jnp.einsum("snd,dhe->shne", a, heads(w), preferred_element_type=jnp.float32)
    own_rows = normed.reshape(seqs, rows, width)
    all_rows = normed_all.reshape(seqs, total, width)
    qh = (project(own_rows, wq) + f32(bq).reshape(H, 1, HD)).astype(jnp.bfloat16)
    kh = project(all_rows, wk).astype(jnp.bfloat16)
    vh = (project(all_rows, wv) + f32(bv).reshape(H, 1, HD)).astype(jnp.bfloat16)
    scale = HD ** (-0.5)
    scores = jnp.einsum("shqd,shkd->shqk", qh, kh, preferred_element_type=jnp.float32) * scale
    valid = positions[None, :] < lengths[:, None]
    scores = jnp.where(valid[:, None, None, :], scores, -1e30)
    top = jnp.max(scores, axis=-1, keepdims=True)
    expd = jnp.exp(scores - top)
    probs = expd / jnp.sum(expd, axis=-1, keepdims=True)
    low_probs = probs.astype(jnp.bfloat16)
    mixed = jnp.einsum("shqk,shkd->sqhd", low_probs, vh, preferred_element_type=jnp.float32)
    mixed = mixed.reshape(n, width).astype(jnp.bfloat16)
    middle = x + mm(mixed, wo) + f32(bo)
    xhat2, rstd2 = row_stats(middle)
    normed_two = (xhat2 * f32(ln2_gain) + f32(ln2_bias)).astype(jnp.bfloat16)
    ffn_pre = mm(normed_two, wi) + f32(bi)
    cdf = 0.5 * (1.0 + lax.erf(ffn_pre * (1.0 / math.sqrt(2.0))))
    ffn_act = (ffn_pre * cdf).astype(jnp.bfloat16)
    result = middle + mm(ffn_act, wf) + f32(bf)
    output = result.astype(jnp.bfloat16).reshape(seqs, rows, width)

    g = f32(out_grad).reshape(n, width)
    g_low = g.astype(jnp.bfloat16)
    grad_bf = col_sum(g_low)
    grad_wf = outer(ffn_act, g_low)
    d_act = back(g_low, wf)
    pdf = jnp.exp(-0.5 * ffn_pre * ffn_pre) * (1.0 / math.sqrt(2.0 * math.pi))
    d_pre = (d_act * (cdf + ffn_pre * pdf)).astype(jnp.bfloat16)
    grad_bi = col_sum(d_pre)
    grad_wi = outer(normed_two, d_pre)
    d_normed_two = back(d_pre, wi)
    d_mid = norm_back_rows(d_normed_two, xhat2, rstd2, f32(ln2_gain))
    grad_ln2_gain = jnp.sum(d_normed_two * xhat2, axis=0)
    grad_ln2_bias = jnp.sum(d_normed_two, axis=0)
    d_middle = g + d_mid
    d_branch = d_middle.astype(jnp.bfloat16)
    grad_bo = col_sum(d_branch)
    grad_wo = outer(mixed, d_branch)
    grads = {
        7: grad_wo, 8: grad_bo, 9: grad_ln2_gain, 10: grad_ln2_bias,
        11: grad_wi, 12: grad_bi, 13: grad_wf, 14: grad_bf,
    }
    early_part = dp_stage(pack_group(grads, EARLY, width, mesh_shape))
    d_mixed = back(d_branch, wo).astype(jnp.bfloat16).reshape(seqs, rows, H, HD)
    d_probs = jnp.einsum("sqhd,shkd->shqk", d_mixed, vh, preferred_element_type=jnp.float32)
    inner = jnp.sum(probs * d_probs, axis=-1, keepdims=True)
    d_scores = (probs * (d_probs - inner)).astype(jnp.bfloat16)
    d_q = jnp.einsum("shqk,shkd->sqhd", d_scores, kh, preferred_element_type=jnp.float32) * scale
    d_q = d_q.reshape(n, width).astype(jnp.bfloat16)
    k_part = (
        jnp.einsum("shqk,shqd->skhd", d_scores, qh, preferred_element_type=jnp.float32) * scale
    ).reshape(seqs * total, width).astype(jnp.bfloat16)
    v_part = jnp.einsum("shqk,sqhd->skhd", low_probs, d_mixed, preferred_element_type=jnp.float32)
    v_part = v_part.reshape(seqs * total, width).astype(jnp.bfloat16)
    grad_bq = col_sum(d_q)
    grad_bv = col_sum(v_part)
    grad_wq = outer(normed, d_q)
    grad_wk = outer(normed_all, k_part)
    grad_wv = outer(normed_all, v_part)
    kv_back = back(k_part, wk) + back(v_part, wv)
    q_back = back(d_q, wq)
    grad_ln1_gain = jnp.sum(kv_back * xhat_all, axis=0) + jnp.sum(q_back * xhat1, axis=0)
    grad_ln1_bias = jnp.sum(kv_back, axis=0) + jnp.sum(q_back, axis=0)

    kv_blocks = kv_back.reshape(seqs, total, width)
    d_normed = kv_blocks[:, :rows] + q_back.reshape(seqs, rows, width)
    for b in range(1, n_ctx):
        sent = kv_blocks[:, b * rows:(b + 1) * rows].astype(jnp.bfloat16)
        got = lax.ppermute(sent, "ctx", [(i, (i - b) % n_ctx) for i in range(n_ctx)])
        d_normed = d_normed + f32(got)

    grads.update({0: grad_ln1_gain, 1: grad_ln1_bias, 2: grad_wq, 3: grad_bq, 4: grad_wk, 5: grad_wv, 6: grad_bv})
    late_part = dp_stage(pack_group(grads, LATE, width, mesh_shape))
    xhat1_b, rstd1_b = lax.optimization_barrier((xhat1, rstd1))
    d_x = norm_back_rows(d_normed.reshape(n, width), xhat1_b, rstd1_b, f32(ln1_gain))
    input_grad = (d_middle + d_x).astype(jnp.bfloat16).reshape(seqs, rows, width)
    early_sum, late_sum = ctx_stage([early_part, late_part])
    out = unpack_group(early_sum, grads, EARLY, width, groups)
    out.update(unpack_group(late_sum, grads, LATE, width, groups))
    return (output, input_grad) + tuple(out[i] for i in range(15))


def solution(mesh):
    row = P(("dp", "ctx"))
    mat = P(("dp", "ctx"), None)
    act = P("dp", "ctx", None)
    weight_specs = (row, row, mat, row, mat, mat, row, mat, row, row, row, mat, row, mat, row)
    return jax.shard_map(
        layer,
        mesh=mesh,
        in_specs=(act, P("dp")) + weight_specs + (act,),
        out_specs=(act, act) + weight_specs,
        check_vma=False,
    )
```

```python
import math

import jax
import jax.numpy as jnp
from jax import lax
from jax.sharding import PartitionSpec as P


H = 12
HD = 64
EPS = 1e-06
ALL = ("dp", "ctx")


def row_stats(rows):
    mean = jnp.mean(rows, axis=-1, keepdims=True)
    center = rows - mean
    rstd = lax.rsqrt(jnp.mean(center * center, axis=-1, keepdims=True) + EPS)
    return center * rstd, rstd


def norm_back_rows(d_normed, xhat, rstd, gain):
    e = d_normed * gain
    mean_e = jnp.mean(e, axis=-1, keepdims=True)
    mean_ex = jnp.mean(e * xhat, axis=-1, keepdims=True)
    return (e - mean_e - xhat * mean_ex) * rstd


def mm(left, right):
    return jnp.dot(left, right, preferred_element_type=jnp.float32)


def outer(left_rows, right_rows):
    return lax.dot_general(
        left_rows, right_rows, (((0,), (0,)), ((), ())), preferred_element_type=jnp.float32
    )


def back(grad_rows, weight):
    return lax.dot_general(
        grad_rows, weight, (((1,), (1,)), ((), ())), preferred_element_type=jnp.float32
    )


def col_sum(rows):
    return jnp.sum(rows.astype(jnp.float32), axis=0)


def round_up(value, step):
    return -(-value // step) * step


def layout(shards, group, width, sub):
    mats = [i for i in group if shards[i].ndim == 2]
    vecs = [i for i in group if shards[i].ndim == 1]
    rows = [shards[i].size // width for i in mats]
    vec_len = sum(shards[i].size for i in vecs)
    vec_rows = round_up(vec_len, width) // width
    total = round_up(sum(rows) + vec_rows, sub)
    return mats, vecs, rows, vec_len, vec_rows, total


def gather_all(shards, group, width, groups):
    mats, vecs, rows, vec_len, vec_rows, total = layout(shards, group, width, 16)
    spare = total - sum(rows) - vec_rows
    vec = jnp.concatenate([shards[i].reshape(-1) for i in vecs])
    vec = jnp.pad(vec, (0, (vec_rows + spare) * width - vec_len)).reshape(vec_rows + spare, width)
    blocks = [shards[i].reshape(-1, width) for i in mats] + [vec]
    packed = jnp.concatenate(blocks, axis=0)
    full = lax.all_gather(packed[None], ALL, axis=0, tiled=True)
    out = {}
    off = 0
    for i, r in zip(mats, rows):
        s = shards[i]
        out[i] = full[:, off:off + r, :].reshape((groups * s.shape[0],) + s.shape[1:])
        off += r
    flat = full[:, off:off + vec_rows, :].reshape(groups, vec_rows * width)
    voff = 0
    for i in vecs:
        size = shards[i].size
        out[i] = flat[:, voff:voff + size].reshape(groups * size)
        voff += size
    return [out[i] for i in group]


LATE_W = (7, 8, 9, 10, 11, 12, 13, 14)


def pack_group(grads, group, width, mesh_shape):
    groups = mesh_shape[0] * mesh_shape[1]
    mats = [i for i in group if grads[i].ndim == 2]
    vecs = [i for i in group if grads[i].ndim == 1]
    rows = [grads[i].size // groups // width for i in mats]
    vec_len = sum(grads[i].size // groups for i in vecs)
    vec_rows = round_up(vec_len, width) // width
    total = round_up(sum(rows) + vec_rows, 16)
    spare = total - sum(rows) - vec_rows
    vec = jnp.concatenate([grads[i].reshape(groups, -1) for i in vecs], axis=1)
    vec = jnp.pad(vec, ((0, 0), (0, (vec_rows + spare) * width - vec_len)))
    vec = vec.reshape(groups, vec_rows + spare, width)
    blocks = [grads[i].reshape(groups, -1, width) for i in mats] + [vec]
    packed = jnp.concatenate([b.astype(jnp.bfloat16) for b in blocks], axis=1)
    return packed.reshape(mesh_shape[0], mesh_shape[1], total, width)


def dp_stage(packed):
    return lax.psum_scatter(packed, "dp", scatter_dimension=0, tiled=True)


def ctx_stage(parts):
    joined = jnp.concatenate(parts, axis=2)
    mine = lax.psum_scatter(joined, "ctx", scatter_dimension=1, tiled=True)
    mine = mine.reshape(joined.shape[2], joined.shape[3]).astype(jnp.float32)
    out, off = [], 0
    for p in parts:
        out.append(mine[off:off + p.shape[2]])
        off += p.shape[2]
    return out


def unpack_group(mine, grads, group, width, groups):
    out = {}
    off = 0
    for i in [i for i in group if grads[i].ndim == 2]:
        shape = (grads[i].shape[0] // groups,) + grads[i].shape[1:]
        r = math.prod(shape) // width
        out[i] = mine[off:off + r, :].reshape(shape)
        off += r
    flat = mine[off:, :].reshape(-1)
    voff = 0
    for i in [i for i in group if grads[i].ndim == 1]:
        size = grads[i].shape[0] // groups
        out[i] = flat[voff:voff + size]
        voff += size
    return out


EARLY = (7, 8, 9, 10, 11, 12, 13, 14)
LATE = (0, 1, 2, 3, 4, 5, 6)


def layer(inputs, lengths, *rest):
    shards = rest[:15]
    out_grad = rest[15]
    n_ctx = lax.axis_size("ctx")
    mesh_shape = (lax.axis_size("dp"), n_ctx)
    groups = mesh_shape[0] * mesh_shape[1]
    seqs, rows, width = inputs.shape
    f32 = lambda a: a.astype(jnp.float32)

    blocks = [inputs]
    for b in range(1, n_ctx):
        blocks.append(lax.ppermute(inputs, "ctx", [(i, (i + b) % n_ctx) for i in range(n_ctx)]))
    first = (0, 1, 2, 3, 4, 5, 6)
    ln1_gain, ln1_bias, wq, bq, wk, wv, bv = gather_all(shards, first, width, groups)
    wo, bo, ln2_gain, ln2_bias, wi, bi, wf, bf = gather_all(shards, LATE_W, width, groups)
    me = lax.axis_index("ctx")
    total = n_ctx * rows
    source = (me - jnp.arange(n_ctx)) % n_ctx
    positions = (source[:, None] * rows + jnp.arange(rows)[None, :]).reshape(total)
    n = seqs * rows

    x_all = f32(jnp.concatenate(blocks, axis=1)).reshape(seqs * total, width)
    xhat_all, rstd_all = row_stats(x_all)
    normed_all = (xhat_all * f32(ln1_gain) + f32(ln1_bias)).astype(jnp.bfloat16)
    own = lambda a: a.reshape(seqs, total, width)[:, :rows].reshape(n, width)
    normed = own(normed_all)
    xhat1 = own(xhat_all)
    rstd1 = rstd_all.reshape(seqs, total, 1)[:, :rows].reshape(n, 1)
    x = f32(inputs).reshape(n, width)
    heads = lambda w: w.reshape(width, H, HD)
    project = lambda a, w: jnp.einsum("snd,dhe->shne", a, heads(w), preferred_element_type=jnp.float32)
    own_rows = normed.reshape(seqs, rows, width)
    all_rows = normed_all.reshape(seqs, total, width)
    qh = (project(own_rows, wq) + f32(bq).reshape(H, 1, HD)).astype(jnp.bfloat16)
    kh = project(all_rows, wk).astype(jnp.bfloat16)
    vh = (project(all_rows, wv) + f32(bv).reshape(H, 1, HD)).astype(jnp.bfloat16)
    scale = HD ** (-0.5)
    scores = jnp.einsum("shqd,shkd->shqk", qh, kh, preferred_element_type=jnp.float32) * scale
    valid = positions[None, :] < lengths[:, None]
    scores = jnp.where(valid[:, None, None, :], scores, -1e30)
    top = jnp.max(scores, axis=-1, keepdims=True)
    expd = jnp.exp(scores - top)
    probs = expd / jnp.sum(expd, axis=-1, keepdims=True)
    low_probs = probs.astype(jnp.bfloat16)
    mixed = jnp.einsum("shqk,shkd->sqhd", low_probs, vh, preferred_element_type=jnp.float32)
    mixed = mixed.reshape(n, width).astype(jnp.bfloat16)
    middle = x + mm(mixed, wo) + f32(bo)
    xhat2, rstd2 = row_stats(middle)
    normed_two = (xhat2 * f32(ln2_gain) + f32(ln2_bias)).astype(jnp.bfloat16)
    ffn_pre = mm(normed_two, wi) + f32(bi)
    cdf = 0.5 * (1.0 + lax.erf(ffn_pre * (1.0 / math.sqrt(2.0))))
    ffn_act = (ffn_pre * cdf).astype(jnp.bfloat16)
    result = middle + mm(ffn_act, wf) + f32(bf)
    output = result.astype(jnp.bfloat16).reshape(seqs, rows, width)

    g = f32(out_grad).reshape(n, width)
    g_low = g.astype(jnp.bfloat16)
    grad_bf = col_sum(g_low)
    grad_wf = outer(ffn_act, g_low)
    d_act = back(g_low, wf)
    pdf = jnp.exp(-0.5 * ffn_pre * ffn_pre) * (1.0 / math.sqrt(2.0 * math.pi))
    d_pre = (d_act * (cdf + ffn_pre * pdf)).astype(jnp.bfloat16)
    grad_bi = col_sum(d_pre)
    grad_wi = outer(normed_two, d_pre)
    d_normed_two = back(d_pre, wi)
    d_mid = norm_back_rows(d_normed_two, xhat2, rstd2, f32(ln2_gain))
    grad_ln2_gain = jnp.sum(d_normed_two * xhat2, axis=0)
    grad_ln2_bias = jnp.sum(d_normed_two, axis=0)
    d_middle = g + d_mid
    d_branch = d_middle.astype(jnp.bfloat16)
    grad_bo = col_sum(d_branch)
    grad_wo = outer(mixed, d_branch)
    grads = {
        7: grad_wo, 8: grad_bo, 9: grad_ln2_gain, 10: grad_ln2_bias,
        11: grad_wi, 12: grad_bi, 13: grad_wf, 14: grad_bf,
    }
    early_part = dp_stage(pack_group(grads, EARLY, width, mesh_shape))
    (early_sum,) = ctx_stage([early_part])
    d_mixed = back(d_branch, wo).astype(jnp.bfloat16).reshape(seqs, rows, H, HD)
    d_probs = jnp.einsum("sqhd,shkd->shqk", d_mixed, vh, preferred_element_type=jnp.float32)
    inner = jnp.sum(probs * d_probs, axis=-1, keepdims=True)
    d_scores = (probs * (d_probs - inner)).astype(jnp.bfloat16)
    d_q = jnp.einsum("shqk,shkd->sqhd", d_scores, kh, preferred_element_type=jnp.float32) * scale
    d_q = d_q.reshape(n, width).astype(jnp.bfloat16)
    k_part = (
        jnp.einsum("shqk,shqd->skhd", d_scores, qh, preferred_element_type=jnp.float32) * scale
    ).reshape(seqs * total, width).astype(jnp.bfloat16)
    v_part = jnp.einsum("shqk,sqhd->skhd", low_probs, d_mixed, preferred_element_type=jnp.float32)
    v_part = v_part.reshape(seqs * total, width).astype(jnp.bfloat16)
    grad_bq = col_sum(d_q)
    grad_bv = col_sum(v_part)
    grad_wq = outer(normed, d_q)
    grad_wk = outer(normed_all, k_part)
    grad_wv = outer(normed_all, v_part)
    kv_back = back(k_part, wk) + back(v_part, wv)
    q_back = back(d_q, wq)
    grad_ln1_gain = jnp.sum(kv_back * xhat_all, axis=0) + jnp.sum(q_back * xhat1, axis=0)
    grad_ln1_bias = jnp.sum(kv_back, axis=0) + jnp.sum(q_back, axis=0)

    kv_blocks = kv_back.reshape(seqs, total, width)
    d_normed = kv_blocks[:, :rows] + q_back.reshape(seqs, rows, width)
    for b in range(1, n_ctx):
        sent = kv_blocks[:, b * rows:(b + 1) * rows].astype(jnp.bfloat16)
        got = lax.ppermute(sent, "ctx", [(i, (i - b) % n_ctx) for i in range(n_ctx)])
        d_normed = d_normed + f32(got)

    grads.update({0: grad_ln1_gain, 1: grad_ln1_bias, 2: grad_wq, 3: grad_bq, 4: grad_wk, 5: grad_wv, 6: grad_bv})
    late_part = dp_stage(pack_group(grads, LATE, width, mesh_shape))
    xhat1_b, rstd1_b = lax.optimization_barrier((xhat1, rstd1))
    d_x = norm_back_rows(d_normed.reshape(n, width), xhat1_b, rstd1_b, f32(ln1_gain))
    input_grad = (d_middle + d_x).astype(jnp.bfloat16).reshape(seqs, rows, width)
    (late_sum,) = ctx_stage([late_part])
    out = unpack_group(early_sum, grads, EARLY, width, groups)
    out.update(unpack_group(late_sum, grads, LATE, width, groups))
    return (output, input_grad) + tuple(out[i] for i in range(15))


def solution(mesh):
    row = P(("dp", "ctx"))
    mat = P(("dp", "ctx"), None)
    act = P("dp", "ctx", None)
    weight_specs = (row, row, mat, row, mat, mat, row, mat, row, row, row, mat, row, mat, row)
    return jax.shard_map(
        layer,
        mesh=mesh,
        in_specs=(act, P("dp")) + weight_specs + (act,),
        out_specs=(act, act) + weight_specs,
        check_vma=False,
    )
```

```python
import math

import jax
import jax.numpy as jnp
from jax import lax
from jax.sharding import PartitionSpec as P


H = 12
HD = 64
EPS = 1e-06
ALL = ("dp", "ctx")


def row_stats(rows):
    mean = jnp.mean(rows, axis=-1, keepdims=True)
    center = rows - mean
    rstd = lax.rsqrt(jnp.mean(center * center, axis=-1, keepdims=True) + EPS)
    return center * rstd, rstd


def norm_back_rows(d_normed, xhat, rstd, gain):
    e = d_normed * gain
    mean_e = jnp.mean(e, axis=-1, keepdims=True)
    mean_ex = jnp.mean(e * xhat, axis=-1, keepdims=True)
    return (e - mean_e - xhat * mean_ex) * rstd


def mm(left, right):
    return jnp.dot(left, right, preferred_element_type=jnp.float32)


def outer(left_rows, right_rows):
    return lax.dot_general(
        left_rows, right_rows, (((0,), (0,)), ((), ())), preferred_element_type=jnp.float32
    )


def back(grad_rows, weight):
    return lax.dot_general(
        grad_rows, weight, (((1,), (1,)), ((), ())), preferred_element_type=jnp.float32
    )


def col_sum(rows):
    return jnp.sum(rows.astype(jnp.float32), axis=0)


def round_up(value, step):
    return -(-value // step) * step


def layout(shards, group, width, sub):
    mats = [i for i in group if shards[i].ndim == 2]
    vecs = [i for i in group if shards[i].ndim == 1]
    rows = [shards[i].size // width for i in mats]
    vec_len = sum(shards[i].size for i in vecs)
    vec_rows = round_up(vec_len, width) // width
    total = round_up(sum(rows) + vec_rows, sub)
    return mats, vecs, rows, vec_len, vec_rows, total


def gather_all(shards, group, width, groups):
    mats, vecs, rows, vec_len, vec_rows, total = layout(shards, group, width, 16)
    spare = total - sum(rows) - vec_rows
    vec = jnp.concatenate([shards[i].reshape(-1) for i in vecs])
    vec = jnp.pad(vec, (0, (vec_rows + spare) * width - vec_len)).reshape(vec_rows + spare, width)
    blocks = [shards[i].reshape(-1, width) for i in mats] + [vec]
    packed = jnp.concatenate(blocks, axis=0)
    full = lax.all_gather(packed[None], ALL, axis=0, tiled=True)
    out = {}
    off = 0
    for i, r in zip(mats, rows):
        s = shards[i]
        out[i] = full[:, off:off + r, :].reshape((groups * s.shape[0],) + s.shape[1:])
        off += r
    flat = full[:, off:off + vec_rows, :].reshape(groups, vec_rows * width)
    voff = 0
    for i in vecs:
        size = shards[i].size
        out[i] = flat[:, voff:voff + size].reshape(groups * size)
        voff += size
    return [out[i] for i in group]


LATE_W = (7, 8, 9, 10, 11, 12, 13, 14)


def pack_group(grads, group, width, mesh_shape):
    groups = mesh_shape[0] * mesh_shape[1]
    mats = [i for i in group if grads[i].ndim == 2]
    vecs = [i for i in group if grads[i].ndim == 1]
    rows = [grads[i].size // groups // width for i in mats]
    vec_len = sum(grads[i].size // groups for i in vecs)
    vec_rows = round_up(vec_len, width) // width
    total = round_up(sum(rows) + vec_rows, 16)
    spare = total - sum(rows) - vec_rows
    vec = jnp.concatenate([grads[i].reshape(groups, -1) for i in vecs], axis=1)
    vec = jnp.pad(vec, ((0, 0), (0, (vec_rows + spare) * width - vec_len)))
    vec = vec.reshape(groups, vec_rows + spare, width)
    blocks = [grads[i].reshape(groups, -1, width) for i in mats] + [vec]
    packed = jnp.concatenate([b.astype(jnp.bfloat16) for b in blocks], axis=1)
    return packed.reshape(mesh_shape[0], mesh_shape[1], total, width)


def dp_stage(packed):
    return lax.psum_scatter(packed, "dp", scatter_dimension=0, tiled=True)


def ctx_stage(parts):
    joined = jnp.concatenate(parts, axis=2)
    mine = lax.psum_scatter(joined, "ctx", scatter_dimension=1, tiled=True)
    mine = mine.reshape(joined.shape[2], joined.shape[3]).astype(jnp.float32)
    out, off = [], 0
    for p in parts:
        out.append(mine[off:off + p.shape[2]])
        off += p.shape[2]
    return out


def unpack_group(mine, grads, group, width, groups):
    out = {}
    off = 0
    for i in [i for i in group if grads[i].ndim == 2]:
        shape = (grads[i].shape[0] // groups,) + grads[i].shape[1:]
        r = math.prod(shape) // width
        out[i] = mine[off:off + r, :].reshape(shape)
        off += r
    flat = mine[off:, :].reshape(-1)
    voff = 0
    for i in [i for i in group if grads[i].ndim == 1]:
        size = grads[i].shape[0] // groups
        out[i] = flat[voff:voff + size]
        voff += size
    return out


EARLY = (7, 8, 9, 10, 11, 12, 13, 14)
LATE = (0, 1, 2, 3, 4, 5, 6)


def layer(inputs, lengths, *rest):
    shards = rest[:15]
    out_grad = rest[15]
    n_ctx = lax.axis_size("ctx")
    mesh_shape = (lax.axis_size("dp"), n_ctx)
    groups = mesh_shape[0] * mesh_shape[1]
    seqs, rows, width = inputs.shape
    f32 = lambda a: a.astype(jnp.float32)

    blocks = [inputs]
    for b in range(1, n_ctx):
        blocks.append(lax.ppermute(inputs, "ctx", [(i, (i + b) % n_ctx) for i in range(n_ctx)]))
    first = (0, 1, 2, 3, 4, 5, 6)
    ln1_gain, ln1_bias, wq, bq, wk, wv, bv = gather_all(shards, first, width, groups)
    wo, bo, ln2_gain, ln2_bias, wi, bi, wf, bf = gather_all(shards, LATE_W, width, groups)
    me = lax.axis_index("ctx")
    total = n_ctx * rows
    source = (me - jnp.arange(n_ctx)) % n_ctx
    positions = (source[:, None] * rows + jnp.arange(rows)[None, :]).reshape(total)
    n = seqs * rows

    x_all = f32(jnp.concatenate(blocks, axis=1)).reshape(seqs * total, width)
    xhat_all, rstd_all = row_stats(x_all)
    normed_all = (xhat_all * f32(ln1_gain) + f32(ln1_bias)).astype(jnp.bfloat16)
    own = lambda a: a.reshape(seqs, total, width)[:, :rows].reshape(n, width)
    normed = own(normed_all)
    xhat1 = own(xhat_all)
    rstd1 = rstd_all.reshape(seqs, total, 1)[:, :rows].reshape(n, 1)
    x = f32(inputs).reshape(n, width)
    heads = lambda w: w.reshape(width, H, HD)
    project = lambda a, w: jnp.einsum("snd,dhe->shne", a, heads(w), preferred_element_type=jnp.float32)
    own_rows = normed.reshape(seqs, rows, width)
    all_rows = normed_all.reshape(seqs, total, width)
    qh = (project(own_rows, wq) + f32(bq).reshape(H, 1, HD)).astype(jnp.bfloat16)
    kh = project(all_rows, wk).astype(jnp.bfloat16)
    vh = (project(all_rows, wv) + f32(bv).reshape(H, 1, HD)).astype(jnp.bfloat16)
    scale = HD ** (-0.5)
    scores = jnp.einsum("shqd,shkd->shqk", qh, kh, preferred_element_type=jnp.float32) * scale
    valid = positions[None, :] < lengths[:, None]
    scores = jnp.where(valid[:, None, None, :], scores, -1e30)
    top = jnp.max(scores, axis=-1, keepdims=True)
    expd = jnp.exp(scores - top)
    probs = expd * (1.0 / jnp.sum(expd, axis=-1, keepdims=True))
    low_probs = probs.astype(jnp.bfloat16)
    mixed = jnp.einsum("shqk,shkd->sqhd", low_probs, vh, preferred_element_type=jnp.float32)
    mixed = mixed.reshape(n, width).astype(jnp.bfloat16)
    middle = x + mm(mixed, wo) + f32(bo)
    xhat2, rstd2 = row_stats(middle)
    normed_two = (xhat2 * f32(ln2_gain) + f32(ln2_bias)).astype(jnp.bfloat16)
    ffn_pre = mm(normed_two, wi) + f32(bi)
    cdf = 0.5 * (1.0 + lax.erf(ffn_pre * (1.0 / math.sqrt(2.0))))
    ffn_act = (ffn_pre * cdf).astype(jnp.bfloat16)
    result = middle + mm(ffn_act, wf) + f32(bf)
    output = result.astype(jnp.bfloat16).reshape(seqs, rows, width)

    g = f32(out_grad).reshape(n, width)
    g_low = g.astype(jnp.bfloat16)
    grad_bf = col_sum(g_low)
    grad_wf = outer(ffn_act, g_low)
    d_act = back(g_low, wf)
    pdf = jnp.exp(-0.5 * ffn_pre * ffn_pre) * (1.0 / math.sqrt(2.0 * math.pi))
    d_pre = (d_act * (cdf + ffn_pre * pdf)).astype(jnp.bfloat16)
    grad_bi = col_sum(d_pre)
    grad_wi = outer(normed_two, d_pre)
    d_normed_two = back(d_pre, wi)
    d_mid = norm_back_rows(d_normed_two, xhat2, rstd2, f32(ln2_gain))
    grad_ln2_gain = jnp.sum(d_normed_two * xhat2, axis=0)
    grad_ln2_bias = jnp.sum(d_normed_two, axis=0)
    d_middle = g + d_mid
    d_branch = d_middle.astype(jnp.bfloat16)
    grad_bo = col_sum(d_branch)
    grad_wo = outer(mixed, d_branch)
    grads = {
        7: grad_wo, 8: grad_bo, 9: grad_ln2_gain, 10: grad_ln2_bias,
        11: grad_wi, 12: grad_bi, 13: grad_wf, 14: grad_bf,
    }
    early_part = dp_stage(pack_group(grads, EARLY, width, mesh_shape))
    d_mixed = back(d_branch, wo).astype(jnp.bfloat16).reshape(seqs, rows, H, HD)
    d_probs = jnp.einsum("sqhd,shkd->shqk", d_mixed, vh, preferred_element_type=jnp.float32)
    inner = jnp.sum(probs * d_probs, axis=-1, keepdims=True)
    d_scores = (probs * (d_probs - inner)).astype(jnp.bfloat16)
    d_q = jnp.einsum("shqk,shkd->sqhd", d_scores, kh, preferred_element_type=jnp.float32) * scale
    d_q = d_q.reshape(n, width).astype(jnp.bfloat16)
    k_part = (
        jnp.einsum("shqk,shqd->skhd", d_scores, qh, preferred_element_type=jnp.float32) * scale
    ).reshape(seqs * total, width).astype(jnp.bfloat16)
    v_part = jnp.einsum("shqk,sqhd->skhd", low_probs, d_mixed, preferred_element_type=jnp.float32)
    v_part = v_part.reshape(seqs * total, width).astype(jnp.bfloat16)
    grad_bq = col_sum(d_q)
    grad_bv = col_sum(v_part)
    grad_wq = outer(normed, d_q)
    grad_wk = outer(normed_all, k_part)
    grad_wv = outer(normed_all, v_part)
    kv_back = back(k_part, wk) + back(v_part, wv)
    q_back = back(d_q, wq)
    grad_ln1_gain = jnp.sum(kv_back * xhat_all, axis=0) + jnp.sum(q_back * xhat1, axis=0)
    grad_ln1_bias = jnp.sum(kv_back, axis=0) + jnp.sum(q_back, axis=0)

    kv_blocks = kv_back.reshape(seqs, total, width)
    d_normed = kv_blocks[:, :rows] + q_back.reshape(seqs, rows, width)
    for b in range(1, n_ctx):
        sent = kv_blocks[:, b * rows:(b + 1) * rows].astype(jnp.bfloat16)
        got = lax.ppermute(sent, "ctx", [(i, (i - b) % n_ctx) for i in range(n_ctx)])
        d_normed = d_normed + f32(got)

    grads.update({0: grad_ln1_gain, 1: grad_ln1_bias, 2: grad_wq, 3: grad_bq, 4: grad_wk, 5: grad_wv, 6: grad_bv})
    late_part = dp_stage(pack_group(grads, LATE, width, mesh_shape))
    xhat1_b, rstd1_b = lax.optimization_barrier((xhat1, rstd1))
    d_x = norm_back_rows(d_normed.reshape(n, width), xhat1_b, rstd1_b, f32(ln1_gain))
    input_grad = (d_middle + d_x).astype(jnp.bfloat16).reshape(seqs, rows, width)
    early_sum, late_sum = ctx_stage([early_part, late_part])
    out = unpack_group(early_sum, grads, EARLY, width, groups)
    out.update(unpack_group(late_sum, grads, LATE, width, groups))
    return (output, input_grad) + tuple(out[i] for i in range(15))


def solution(mesh):
    row = P(("dp", "ctx"))
    mat = P(("dp", "ctx"), None)
    act = P("dp", "ctx", None)
    weight_specs = (row, row, mat, row, mat, mat, row, mat, row, row, row, mat, row, mat, row)
    return jax.shard_map(
        layer,
        mesh=mesh,
        in_specs=(act, P("dp")) + weight_specs + (act,),
        out_specs=(act, act) + weight_specs,
        check_vma=False,
    )
```

```python
import math

import jax
import jax.numpy as jnp
from jax import lax
from jax.sharding import PartitionSpec as P


H = 12
HD = 64
EPS = 1e-06
ALL = ("dp", "ctx")


def row_stats(rows):
    mean = jnp.mean(rows, axis=-1, keepdims=True)
    center = rows - mean
    rstd = lax.rsqrt(jnp.mean(center * center, axis=-1, keepdims=True) + EPS)
    return center * rstd, rstd


def norm_back_rows(d_normed, xhat, rstd, gain):
    e = d_normed * gain
    mean_e = jnp.mean(e, axis=-1, keepdims=True)
    mean_ex = jnp.mean(e * xhat, axis=-1, keepdims=True)
    return (e - mean_e - xhat * mean_ex) * rstd


def mm(left, right):
    return jnp.dot(left, right, preferred_element_type=jnp.float32)


def outer(left_rows, right_rows):
    return lax.dot_general(
        left_rows, right_rows, (((0,), (0,)), ((), ())), preferred_element_type=jnp.float32
    )


def back(grad_rows, weight):
    return lax.dot_general(
        grad_rows, weight, (((1,), (1,)), ((), ())), preferred_element_type=jnp.float32
    )


def col_sum(rows):
    return jnp.sum(rows.astype(jnp.float32), axis=0)


def round_up(value, step):
    return -(-value // step) * step


def layout(shards, group, width, sub):
    mats = [i for i in group if shards[i].ndim == 2]
    vecs = [i for i in group if shards[i].ndim == 1]
    rows = [shards[i].size // width for i in mats]
    vec_len = sum(shards[i].size for i in vecs)
    vec_rows = round_up(vec_len, width) // width
    total = round_up(sum(rows) + vec_rows, sub)
    return mats, vecs, rows, vec_len, vec_rows, total


def gather_all(shards, group, width, groups):
    mats, vecs, rows, vec_len, vec_rows, total = layout(shards, group, width, 16)
    spare = total - sum(rows) - vec_rows
    vec = jnp.concatenate([shards[i].reshape(-1) for i in vecs])
    vec = jnp.pad(vec, (0, (vec_rows + spare) * width - vec_len)).reshape(vec_rows + spare, width)
    blocks = [shards[i].reshape(-1, width) for i in mats] + [vec]
    packed = jnp.concatenate(blocks, axis=0)
    full = lax.all_gather(packed[None], ALL, axis=0, tiled=True)
    out = {}
    off = 0
    for i, r in zip(mats, rows):
        s = shards[i]
        out[i] = full[:, off:off + r, :].reshape((groups * s.shape[0],) + s.shape[1:])
        off += r
    flat = full[:, off:off + vec_rows, :].reshape(groups, vec_rows * width)
    voff = 0
    for i in vecs:
        size = shards[i].size
        out[i] = flat[:, voff:voff + size].reshape(groups * size)
        voff += size
    return [out[i] for i in group]


LATE_W = (7, 8, 9, 10, 11, 12, 13, 14)


def pack_group(grads, group, width, mesh_shape):
    groups = mesh_shape[0] * mesh_shape[1]
    mats = [i for i in group if grads[i].ndim == 2]
    vecs = [i for i in group if grads[i].ndim == 1]
    rows = [grads[i].size // groups // width for i in mats]
    vec_len = sum(grads[i].size // groups for i in vecs)
    vec_rows = round_up(vec_len, width) // width
    total = round_up(sum(rows) + vec_rows, 16)
    spare = total - sum(rows) - vec_rows
    vec = jnp.concatenate([grads[i].reshape(groups, -1) for i in vecs], axis=1)
    vec = jnp.pad(vec, ((0, 0), (0, (vec_rows + spare) * width - vec_len)))
    vec = vec.reshape(groups, vec_rows + spare, width)
    blocks = [grads[i].reshape(groups, -1, width) for i in mats] + [vec]
    packed = jnp.concatenate([b.astype(jnp.bfloat16) for b in blocks], axis=1)
    return packed.reshape(mesh_shape[0], mesh_shape[1], total, width)


def dp_stage(packed):
    return lax.psum_scatter(packed, "dp", scatter_dimension=0, tiled=True)


def ctx_stage(parts):
    joined = jnp.concatenate(parts, axis=2)
    mine = lax.psum_scatter(joined, "ctx", scatter_dimension=1, tiled=True)
    mine = mine.reshape(joined.shape[2], joined.shape[3]).astype(jnp.float32)
    out, off = [], 0
    for p in parts:
        out.append(mine[off:off + p.shape[2]])
        off += p.shape[2]
    return out


def unpack_group(mine, grads, group, width, groups):
    out = {}
    off = 0
    for i in [i for i in group if grads[i].ndim == 2]:
        shape = (grads[i].shape[0] // groups,) + grads[i].shape[1:]
        r = math.prod(shape) // width
        out[i] = mine[off:off + r, :].reshape(shape)
        off += r
    flat = mine[off:, :].reshape(-1)
    voff = 0
    for i in [i for i in group if grads[i].ndim == 1]:
        size = grads[i].shape[0] // groups
        out[i] = flat[voff:voff + size]
        voff += size
    return out


EARLY = (7, 8, 9, 10, 11, 12, 13, 14)
LATE = (0, 1, 2, 3, 4, 5, 6)


def layer(inputs, lengths, *rest):
    shards = rest[:15]
    out_grad = rest[15]
    n_ctx = lax.axis_size("ctx")
    mesh_shape = (lax.axis_size("dp"), n_ctx)
    groups = mesh_shape[0] * mesh_shape[1]
    seqs, rows, width = inputs.shape
    f32 = lambda a: a.astype(jnp.float32)

    blocks = [inputs]
    for b in range(1, n_ctx):
        blocks.append(lax.ppermute(inputs, "ctx", [(i, (i + b) % n_ctx) for i in range(n_ctx)]))
    first = (0, 1, 2, 3, 4, 5, 6)
    ln1_gain, ln1_bias, wq, bq, wk, wv, bv = gather_all(shards, first, width, groups)
    wo, bo, ln2_gain, ln2_bias, wi, bi, wf, bf = gather_all(shards, LATE_W, width, groups)
    me = lax.axis_index("ctx")
    total = n_ctx * rows
    source = (me - jnp.arange(n_ctx)) % n_ctx
    positions = (source[:, None] * rows + jnp.arange(rows)[None, :]).reshape(total)
    n = seqs * rows

    x_all = f32(jnp.concatenate(blocks, axis=1)).reshape(seqs * total, width)
    xhat_all, rstd_all = row_stats(x_all)
    normed_all = (xhat_all * f32(ln1_gain) + f32(ln1_bias)).astype(jnp.bfloat16)
    own = lambda a: a.reshape(seqs, total, width)[:, :rows].reshape(n, width)
    normed = own(normed_all)
    xhat1 = own(xhat_all)
    rstd1 = rstd_all.reshape(seqs, total, 1)[:, :rows].reshape(n, 1)
    x = f32(inputs).reshape(n, width)
    heads = lambda w: w.reshape(width, H, HD)
    project = lambda a, w: jnp.einsum("snd,dhe->shne", a, heads(w), preferred_element_type=jnp.float32)
    own_rows = normed.reshape(seqs, rows, width)
    all_rows = normed_all.reshape(seqs, total, width)
    qh = (project(own_rows, wq) + f32(bq).reshape(H, 1, HD)).astype(jnp.bfloat16)
    kh = project(all_rows, wk).astype(jnp.bfloat16)
    vh = (project(all_rows, wv) + f32(bv).reshape(H, 1, HD)).astype(jnp.bfloat16)
    scale = HD ** (-0.5)
    qh_scaled = qh * jnp.asarray(scale, jnp.bfloat16)
    scores = jnp.einsum("shqd,shkd->shqk", qh_scaled, kh, preferred_element_type=jnp.float32)
    valid = positions[None, :] < lengths[:, None]
    scores = jnp.where(valid[:, None, None, :], scores, -1e30)
    top = jnp.max(scores, axis=-1, keepdims=True)
    expd = jnp.exp(scores - top)
    probs = expd / jnp.sum(expd, axis=-1, keepdims=True)
    low_probs = probs.astype(jnp.bfloat16)
    mixed = jnp.einsum("shqk,shkd->sqhd", low_probs, vh, preferred_element_type=jnp.float32)
    mixed = mixed.reshape(n, width).astype(jnp.bfloat16)
    middle = x + mm(mixed, wo) + f32(bo)
    xhat2, rstd2 = row_stats(middle)
    normed_two = (xhat2 * f32(ln2_gain) + f32(ln2_bias)).astype(jnp.bfloat16)
    ffn_pre = mm(normed_two, wi) + f32(bi)
    cdf = 0.5 * (1.0 + lax.erf(ffn_pre * (1.0 / math.sqrt(2.0))))
    ffn_act = (ffn_pre * cdf).astype(jnp.bfloat16)
    result = middle + mm(ffn_act, wf) + f32(bf)
    output = result.astype(jnp.bfloat16).reshape(seqs, rows, width)

    g = f32(out_grad).reshape(n, width)
    g_low = g.astype(jnp.bfloat16)
    grad_bf = col_sum(g_low)
    grad_wf = outer(ffn_act, g_low)
    d_act = back(g_low, wf)
    pdf = jnp.exp(-0.5 * ffn_pre * ffn_pre) * (1.0 / math.sqrt(2.0 * math.pi))
    d_pre = (d_act * (cdf + ffn_pre * pdf)).astype(jnp.bfloat16)
    grad_bi = col_sum(d_pre)
    grad_wi = outer(normed_two, d_pre)
    d_normed_two = back(d_pre, wi)
    d_mid = norm_back_rows(d_normed_two, xhat2, rstd2, f32(ln2_gain))
    grad_ln2_gain = jnp.sum(d_normed_two * xhat2, axis=0)
    grad_ln2_bias = jnp.sum(d_normed_two, axis=0)
    d_middle = g + d_mid
    d_branch = d_middle.astype(jnp.bfloat16)
    grad_bo = col_sum(d_branch)
    grad_wo = outer(mixed, d_branch)
    grads = {
        7: grad_wo, 8: grad_bo, 9: grad_ln2_gain, 10: grad_ln2_bias,
        11: grad_wi, 12: grad_bi, 13: grad_wf, 14: grad_bf,
    }
    early_part = dp_stage(pack_group(grads, EARLY, width, mesh_shape))
    d_mixed = back(d_branch, wo).astype(jnp.bfloat16).reshape(seqs, rows, H, HD)
    d_probs = jnp.einsum("sqhd,shkd->shqk", d_mixed, vh, preferred_element_type=jnp.float32)
    inner = jnp.sum(probs * d_probs, axis=-1, keepdims=True)
    d_scores = (probs * (d_probs - inner)).astype(jnp.bfloat16)
    d_q = jnp.einsum("shqk,shkd->sqhd", d_scores, kh, preferred_element_type=jnp.float32) * scale
    d_q = d_q.reshape(n, width).astype(jnp.bfloat16)
    k_part = (
        jnp.einsum("shqk,shqd->skhd", d_scores, qh_scaled, preferred_element_type=jnp.float32)
    ).reshape(seqs * total, width).astype(jnp.bfloat16)
    v_part = jnp.einsum("shqk,sqhd->skhd", low_probs, d_mixed, preferred_element_type=jnp.float32)
    v_part = v_part.reshape(seqs * total, width).astype(jnp.bfloat16)
    grad_bq = col_sum(d_q)
    grad_bv = col_sum(v_part)
    grad_wq = outer(normed, d_q)
    grad_wk = outer(normed_all, k_part)
    grad_wv = outer(normed_all, v_part)
    kv_back = back(k_part, wk) + back(v_part, wv)
    q_back = back(d_q, wq)
    grad_ln1_gain = jnp.sum(kv_back * xhat_all, axis=0) + jnp.sum(q_back * xhat1, axis=0)
    grad_ln1_bias = jnp.sum(kv_back, axis=0) + jnp.sum(q_back, axis=0)

    kv_blocks = kv_back.reshape(seqs, total, width)
    d_normed = kv_blocks[:, :rows] + q_back.reshape(seqs, rows, width)
    for b in range(1, n_ctx):
        sent = kv_blocks[:, b * rows:(b + 1) * rows].astype(jnp.bfloat16)
        got = lax.ppermute(sent, "ctx", [(i, (i - b) % n_ctx) for i in range(n_ctx)])
        d_normed = d_normed + f32(got)

    grads.update({0: grad_ln1_gain, 1: grad_ln1_bias, 2: grad_wq, 3: grad_bq, 4: grad_wk, 5: grad_wv, 6: grad_bv})
    late_part = dp_stage(pack_group(grads, LATE, width, mesh_shape))
    xhat1_b, rstd1_b = lax.optimization_barrier((xhat1, rstd1))
    d_x = norm_back_rows(d_normed.reshape(n, width), xhat1_b, rstd1_b, f32(ln1_gain))
    input_grad = (d_middle + d_x).astype(jnp.bfloat16).reshape(seqs, rows, width)
    early_sum, late_sum = ctx_stage([early_part, late_part])
    out = unpack_group(early_sum, grads, EARLY, width, groups)
    out.update(unpack_group(late_sum, grads, LATE, width, groups))
    return (output, input_grad) + tuple(out[i] for i in range(15))


def solution(mesh):
    row = P(("dp", "ctx"))
    mat = P(("dp", "ctx"), None)
    act = P("dp", "ctx", None)
    weight_specs = (row, row, mat, row, mat, mat, row, mat, row, row, row, mat, row, mat, row)
    return jax.shard_map(
        layer,
        mesh=mesh,
        in_specs=(act, P("dp")) + weight_specs + (act,),
        out_specs=(act, act) + weight_specs,
        check_vma=False,
    )
```
